32 devices in a mesh: seq: 8 (over z, core), tp: 4 (over y, x).
Axes of the slice: x: 2, y: 2, z: 4, core: 2. Of those that a mesh axis runs over, the one named last changes fastest.
Arguments:
- tokens: bfloat16 [8, 512, 2048], P('seq', None, 'tp'), may hold values from -6 to 6
- segment_ids: int32 [8, 512], P('seq'), may hold values from 0 to 15, as said below
- shard_map: int32 [32], replicated, may hold values from 0 to 31, each once
- trainer_qkv: float32 [2, 2048, 6144], P(None, ('seq', 'tp')), may hold values from -0.125 to 0.125
- trainer_up: float32 [2, 2048, 8192], P(None, ('seq', 'tp')), may hold values from -0.125 to 0.125
- qkv_bias: bfloat16 [2, 6144], P(None, 'tp'), may hold values from -4 to 4
- up_bias: bfloat16 [2, 8192], P(None, 'tp'), may hold values from -3 to 3
- dense_w: bfloat16 [2, 2048, 2048], P(None, 'tp'), may hold values from -0.125 to 0.125
- down_w: bfloat16 [2, 8192, 2048], P(None, 'tp'), may hold values from -0.0625 to 0.0625
- out_bias: float32 [2, 2048], P(None, 'tp'), may hold values from -3 to 3
- norm_gain: float32 [2, 2, 2048], replicated, may hold values from 0.1 to 1.9
- norm_shift: float32 [2, 2, 2048], replicated, may hold values from -3 to 3
Outputs:
- result: bfloat16 [8, 512, 2048], P('seq', None, 'tp')
The draws below stay inside these ranges and needn't reach their ends.
Inputs may be any that keep to these rules, and one draw needn't show every extreme that they name: `shard_map`: each trainer shard number appears exactly once. `segment_ids`: along a row the numbers start at 0 and rise by 0 or 1 from token to token; a row holds one prompt of 512 tokens or several packed prompts.
All inputs are finite; a program needn't handle non-finite values.
Results may differ from the reference program's by a relative error of at most 0.015.
Values may be sent and summed in bfloat16 or wider, within the bound.
No kernel may reach another device: no remote copies, remote signals or barrier semaphores. Data moves between devices by JAX's collectives and lax.ppermute only.
A program may use at most 192 MiB of HBM per device.

```python
import jax
import jax.numpy as jnp
from jax import lax

D = 2048
HEADS = 8
HD = 256
FF = 8192
ROT = 64
LAYERS = 2
L = 512
ROWS = 8
RB = 64
N_TP = 4
DEVICES = 32


def draw_segment_ids(key, part):
    key_kind = jax.random.fold_in(key, 11)
    key_cut = jax.random.fold_in(key, 12)
    key_force = jax.random.fold_in(key, 13)
    key_dense = jax.random.fold_in(key, 14)
    whole_rows = jax.random.randint(key_kind, (ROWS, 1), 0, 2)
    forced = jax.random.randint(key_force, (), 0, ROWS)
    dense = (forced + 1 + jax.random.randint(key_dense, (), 0, ROWS - 1)) % ROWS
    row_index = jnp.arange(ROWS)
    whole_rows = jnp.maximum(whole_rows, (row_index == forced).astype(jnp.int32)[:, None])
    whole_rows = whole_rows * (row_index != dense).astype(jnp.int32)[:, None]
    cuts = (jax.random.randint(key_cut, (ROWS, L), 0, 48) == 0).astype(jnp.int32)
    step = L // 16
    regular = (jnp.arange(L) % step == 0).astype(jnp.int32)
    cuts = jnp.maximum(cuts, regular[None, :] * (row_index == dense).astype(jnp.int32)[:, None])
    cuts = cuts * (jnp.arange(L) > 0).astype(jnp.int32)[None, :]
    cuts = cuts * (1 - whole_rows)
    return jnp.minimum(jnp.cumsum(cuts, axis=1), 15).astype(jnp.int32)


def draw_qkv_bias(key, part):
    key_base = jax.random.fold_in(key, 21)
    base = jnp.clip(0.5 * jax.random.normal(key_base, (LAYERS, 3 * D), jnp.float32), -3.0, 3.0)
    return base.astype(jnp.bfloat16)


def shard_levels(rng, extent, cuts, smallest, largest):
    def one(axis_at, shards_of):
        draws = jax.random.uniform(jax.random.fold_in(jax.random.fold_in(rng, 6), axis_at), (shards_of,), jnp.float32, smallest / len(cuts), largest / len(cuts))
        return jnp.repeat(jnp.exp(draws), extent[axis_at] // shards_of).reshape((-1,) + (1,) * (len(extent) - axis_at - 1))

    level = one(*cuts[0])
    for cut in cuts[1:]:
        level = level * one(*cut)
    return level


def scatter_about(stream_key, dims, deviation, most, split=(), kind=jnp.bfloat16):
    loudness = shard_levels(stream_key, dims, split, -0.22, 0.18) if split else 1.0
    array = jax.random.normal(stream_key, dims, jnp.float32) * deviation * loudness
    return jnp.minimum(jnp.maximum(array, -most), most).astype(kind)


def setup_inputs(seed: int = 0) -> dict:
    splits = jax.random.split(jax.random.key(seed), 13)
    return {
        "tokens": scatter_about(splits[0], (ROWS, L, D), 1.0, 6.0, ((0, 8), (2, 4))),
        "segment_ids": draw_segment_ids(jax.random.fold_in(splits[12], 71), 0),
        "shard_map": jax.random.permutation(splits[2], DEVICES).astype(jnp.int32),
        "trainer_qkv": scatter_about(splits[3], (LAYERS, D, 3 * D), D ** -0.5, 0.125, ((1, 32),), jnp.float32),
        "trainer_up": scatter_about(splits[4], (LAYERS, D, FF), D ** -0.5, 0.125, ((1, 32),), jnp.float32),
        "qkv_bias": draw_qkv_bias(jax.random.fold_in(splits[12], 71), 0),
        "up_bias": scatter_about(splits[6], (LAYERS, FF), 0.5, 3.0, ((1, 4),)),
        "dense_w": scatter_about(splits[7], (LAYERS, D, D), D ** -0.5, 0.125, ((1, 4),)),
        "down_w": scatter_about(splits[8], (LAYERS, FF, D), FF ** -0.5, 0.0625, ((1, 4),)),
        "out_bias": scatter_about(splits[9], (LAYERS, D), 0.4, 3.0, ((1, 4),), jnp.float32),
        "norm_gain": jnp.clip(1.0 + 0.18 * jax.random.normal(splits[10], (LAYERS, 2, D), jnp.float32), 0.1, 1.9),
        "norm_shift": scatter_about(splits[11], (LAYERS, 2, D), 0.4, 3.0, (), jnp.float32),
    }


def layer_norm(values, gain, shift):
    mean = lax.optimization_barrier(jnp.mean(values, axis=-1, keepdims=True))
    centred = values - mean
    var = lax.optimization_barrier(jnp.mean(centred * centred, axis=-1, keepdims=True))
    return centred * lax.rsqrt(var + 1e-05) * gain + shift

def positions(segs):
    length = segs.shape[-1]
    index = jnp.broadcast_to(jnp.arange(length, dtype=jnp.int32), segs.shape)
    first = jnp.ones(segs.shape[:-1] + (1,), dtype=bool)
    flag = jnp.concatenate([first, segs[..., 1:] != segs[..., :-1]], axis=-1)
    start = lax.cummax(jnp.where(flag, index, 0), axis=segs.ndim - 1)
    return index - start

def rotate(values, pos):
    half = ROT // 2
    inverse = 10000.0 ** (-(jnp.arange(half, dtype=jnp.float32) * 2.0 / ROT))
    angle = pos[..., None].astype(jnp.float32) * inverse
    cosine = jnp.cos(angle)[..., None, :]
    sine = jnp.sin(angle)[..., None, :]
    first = values[..., :half]
    second = values[..., half:ROT]
    return jnp.concatenate([first * cosine - second * sine, second * cosine + first * sine, values[..., ROT:]], axis=-1)

def reference(tokens, segment_ids, shard_map, trainer_qkv, trainer_up, qkv_bias, up_bias, dense_w, down_w, out_bias, norm_gain, norm_shift):
    server_qkv = []
    server_up = []
    for layer in range(LAYERS):
        blocks = trainer_qkv[layer].reshape(DEVICES, RB, 3 * D)
        placed = jnp.zeros_like(blocks).at[shard_map].set(blocks)
        server_qkv.append(placed.reshape(D, 3 * D).astype(jnp.bfloat16))
        blocks = trainer_up[layer].reshape(DEVICES, RB, FF)
        placed = jnp.zeros_like(blocks).at[shard_map].set(blocks)
        server_up.append(placed.reshape(D, FF).astype(jnp.bfloat16))
    heads_group = HEADS // N_TP
    cols_group = 3 * D // N_TP
    ff_group = FF // N_TP

    def one_row(item):
        stream, segs = item
        pos = positions(segs)
        index = jnp.arange(L, dtype=jnp.int32)
        mask = (index[None, :] <= index[:, None]) & (segs[:, None] == segs[None, :])
        for layer in range(LAYERS):
            flt = stream.astype(jnp.float32)
            attn_in = layer_norm(flt, norm_gain[layer, 0], norm_shift[layer, 0]).astype(jnp.bfloat16)
            mlp_in = layer_norm(flt, norm_gain[layer, 1], norm_shift[layer, 1]).astype(jnp.bfloat16)
            total = jnp.zeros((L, D), jnp.float32)
            for group in range(N_TP):
                wq = server_qkv[layer][:, group * cols_group:(group + 1) * cols_group]
                qkv = jnp.dot(attn_in, wq, preferred_element_type=jnp.float32)
                qkv = qkv + qkv_bias[layer, group * cols_group:(group + 1) * cols_group].astype(jnp.float32)
                qkv = qkv.reshape(L, heads_group, 3, HD)
                query = rotate(qkv[:, :, 0], pos).astype(jnp.bfloat16)
                keys = rotate(qkv[:, :, 1], pos).astype(jnp.bfloat16)
                vals = qkv[:, :, 2].astype(jnp.bfloat16)
                scores = jnp.einsum('qhd,khd->hqk', query.astype(jnp.float32), keys.astype(jnp.float32)) / jnp.sqrt(jnp.float32(HD))
                scores = jnp.where(mask[None], scores, -jnp.inf)
                probs = jax.nn.softmax(scores, axis=-1).astype(jnp.bfloat16)
                ctx = jnp.einsum('hqk,khd->qhd', probs.astype(jnp.float32), vals.astype(jnp.float32)).astype(jnp.bfloat16)
                ctx = ctx.reshape(L, heads_group * HD)
                up = jnp.dot(mlp_in, server_up[layer][:, group * ff_group:(group + 1) * ff_group], preferred_element_type=jnp.float32)
                up = up + up_bias[layer, group * ff_group:(group + 1) * ff_group].astype(jnp.float32)
                hidden_units = jax.nn.gelu(up, approximate=False).astype(jnp.bfloat16)
                rows_attn = dense_w[layer, group * heads_group * HD:(group + 1) * heads_group * HD]
                rows_mlp = down_w[layer, group * ff_group:(group + 1) * ff_group]
                part = jnp.dot(ctx, rows_attn, preferred_element_type=jnp.float32) + jnp.dot(hidden_units, rows_mlp, preferred_element_type=jnp.float32)
                part = lax.optimization_barrier(part.astype(jnp.bfloat16))
                total = total + part.astype(jnp.float32)
            stream = (flt + total + out_bias[layer]).astype(jnp.bfloat16)
        return stream
    return lax.map(one_row, (tokens, segment_ids))
```

```python
import jax
import jax.numpy as jnp
import numpy as np
from jax import lax
from jax.sharding import Mesh
from jax.sharding import PartitionSpec as P

HD = 256
ROT = 64
LAYERS = 2
HEADS = 8


def layer_norm(values, gain, shift):
    mean = jnp.mean(values, axis=-1, keepdims=True)
    centred = values - mean
    var = jnp.mean(centred * centred, axis=-1, keepdims=True)
    return centred * lax.rsqrt(var + 1e-05) * gain + shift


def positions(segs):
    length = segs.shape[-1]
    index = jnp.broadcast_to(jnp.arange(length, dtype=jnp.int32), segs.shape)
    first = jnp.ones(segs.shape[:-1] + (1,), dtype=bool)
    flag = jnp.concatenate([first, segs[..., 1:] != segs[..., :-1]], axis=-1)
    start = lax.cummax(jnp.where(flag, index, 0), axis=segs.ndim - 1)
    return index - start


def rotate(values, pos):
    half = ROT // 2
    inverse = 10000.0 ** (-(jnp.arange(half, dtype=jnp.float32) * 2.0 / ROT))
    angle = pos[..., None].astype(jnp.float32) * inverse
    cosine = jnp.cos(angle)[..., None, :]
    sine = jnp.sin(angle)[..., None, :]
    first = values[..., :half]
    second = values[..., half:ROT]
    return jnp.concatenate(
        [first * cosine - second * sine, second * cosine + first * sine, values[..., ROT:]], axis=-1
    )


def attention(qkv, pos, mask):
    query = rotate(qkv[:, :, :, 0], pos).astype(jnp.bfloat16)
    keys = rotate(qkv[:, :, :, 1], pos).astype(jnp.bfloat16)
    vals = qkv[:, :, :, 2].astype(jnp.bfloat16)
    scores = jnp.einsum("rqhd,rkhd->rhqk", query, keys, preferred_element_type=jnp.float32) / jnp.sqrt(
        jnp.float32(HD)
    )
    scores = jnp.where(mask, scores, -jnp.inf)
    probs = jax.nn.softmax(scores, axis=-1).astype(jnp.bfloat16)
    ctx = jnp.einsum("rhqk,rkhd->rqhd", probs, vals, preferred_element_type=jnp.float32)
    return ctx.astype(jnp.bfloat16)


def shards(
    tokens,
    segment_ids,
    shard_map,
    trainer_qkv,
    trainer_up,
    qkv_bias,
    up_bias,
    dense_w,
    down_w,
    out_bias,
    norm_gain,
    norm_shift,
):
    n_zz = lax.axis_size("zz")
    n_core = lax.axis_size("core")
    n_tp = lax.axis_size("tp")
    core = lax.axis_index("core")
    _, length, _ = tokens.shape
    block = trainer_qkv.shape[1]
    full_width = trainer_qkv.shape[1] * n_zz * n_core * n_tp
    n_blocks = full_width // block
    heads_group = qkv_bias.shape[1] // (3 * HD)
    ff_group = up_bias.shape[1]
    ff_here = ff_group // n_core
    split_heads = heads_group % n_core == 0
    heads_here = heads_group // n_core if split_heads else heads_group
    qkv_cols = heads_here * 3 * HD
    n_dest = n_tp * n_core

    wq = trainer_qkv.astype(jnp.bfloat16)
    wu = trainer_up.astype(jnp.bfloat16)
    if split_heads:
        wq = wq.reshape(LAYERS, block, n_dest, qkv_cols)
    else:
        wq = wq.reshape(LAYERS, block, n_tp, 1, qkv_cols)
        wq = jnp.broadcast_to(wq, (LAYERS, block, n_tp, n_core, qkv_cols))
        wq = wq.reshape(LAYERS, block, n_dest, qkv_cols)
    wu = wu.reshape(LAYERS, block, n_dest, ff_here)
    packed = jnp.concatenate([wq, wu], axis=-1)
    packed = lax.all_to_all(packed, ("tp", "core"), split_axis=2, concat_axis=1, tiled=True)

    zz_i, t_i, c_i = np.meshgrid(np.arange(n_zz), np.arange(n_tp), np.arange(n_core), indexing="ij")
    source = ((zz_i * n_core + c_i) * n_tp + t_i).reshape(-1)
    feature_block = jnp.take(shard_map, jnp.asarray(source, dtype=jnp.int32))

    segs = lax.all_gather(segment_ids, "core", axis=0, tiled=True)
    rows = segs.shape[0]
    pos = positions(segs)
    index = jnp.arange(length, dtype=jnp.int32)
    mask = (index[None, :] <= index[:, None])[None] & (segs[:, :, None] == segs[:, None, :])
    mask = mask[:, None]
    bias_full = lax.all_gather(out_bias, "tp", axis=1, tiled=True)

    stream = lax.all_gather(tokens, "tp", axis=2, tiled=True)
    stream = lax.all_gather(stream, "core", axis=0, tiled=True)
    for layer in range(LAYERS):
        weights = lax.all_gather(packed[layer].reshape(n_dest * block, -1), "zz", axis=0, tiled=True)
        w_qkv = weights[:, :qkv_cols]
        w_up = weights[:, qkv_cols:]
        flt = stream.astype(jnp.float32)
        permuted = jnp.take(stream.reshape(rows, length, n_blocks, block), feature_block, axis=2)
        permuted = permuted.reshape(rows * length, full_width).astype(jnp.float32)

        def norm_of(i):
            gain = jnp.take(norm_gain[layer, i].reshape(n_blocks, block), feature_block, axis=0)
            shift = jnp.take(norm_shift[layer, i].reshape(n_blocks, block), feature_block, axis=0)
            return layer_norm(permuted, gain.reshape(-1), shift.reshape(-1)).astype(jnp.bfloat16)

        attn_in = norm_of(0)
        mlp_in = norm_of(1)

        if split_heads:
            q_bias = lax.dynamic_slice_in_dim(qkv_bias[layer], core * qkv_cols, qkv_cols)
            qkv = jnp.dot(attn_in, w_qkv, preferred_element_type=jnp.float32) + q_bias.astype(jnp.float32)
            ctx = attention(qkv.reshape(rows, length, heads_here, 3, HD), pos, mask)
            ctx = ctx.reshape(rows * length, heads_here * HD)
            d_rows = lax.dynamic_slice_in_dim(dense_w[layer], core * heads_here * HD, heads_here * HD)
            attn_out = jnp.dot(ctx, d_rows, preferred_element_type=jnp.float32)
        else:
            own = lax.dynamic_slice_in_dim(attn_in.reshape(rows, length, -1), core, 1, axis=0)
            qkv = jnp.dot(own.reshape(length, -1), w_qkv, preferred_element_type=jnp.float32)
            qkv = qkv + qkv_bias[layer].astype(jnp.float32)
            own_pos = lax.dynamic_slice_in_dim(pos, core, 1, axis=0)
            own_mask = lax.dynamic_slice_in_dim(mask, core, 1, axis=0)
            ctx = attention(qkv.reshape(1, length, heads_here, 3, HD), own_pos, own_mask)
            attn_out = jnp.dot(ctx.reshape(length, -1), dense_w[layer], preferred_element_type=jnp.float32)
            here = (jnp.arange(rows) == core)[:, None, None]
            attn_out = jnp.where(here, attn_out[None], 0.0).reshape(rows * length, -1)

        u_bias = lax.dynamic_slice_in_dim(up_bias[layer], core * ff_here, ff_here)
        up = jnp.dot(mlp_in, w_up, preferred_element_type=jnp.float32) + u_bias.astype(jnp.float32)
        hidden_units = jax.nn.gelu(up, approximate=False).astype(jnp.bfloat16)
        m_rows = lax.dynamic_slice_in_dim(down_w[layer], core * ff_here, ff_here)
        partial_terms = attn_out + jnp.dot(hidden_units, m_rows, preferred_element_type=jnp.float32)
        partial_terms = partial_terms.astype(jnp.bfloat16).reshape(rows, length, full_width)
        if layer + 1 < LAYERS:
            summed = lax.psum(partial_terms, ("core", "tp")).astype(jnp.float32)
            stream = (flt + summed + bias_full[layer]).astype(jnp.bfloat16)
        else:
            summed = lax.psum_scatter(partial_terms, "core", scatter_dimension=0, tiled=True)
            summed = lax.psum_scatter(summed, "tp", scatter_dimension=2, tiled=True).astype(jnp.float32)
            width_here = full_width // n_tp
            own_stream = lax.dynamic_slice_in_dim(flt, core, 1, axis=0)
            own_stream = lax.dynamic_slice_in_dim(own_stream, lax.axis_index("tp") * width_here, width_here, axis=2)
            stream = (own_stream + summed + out_bias[layer]).astype(jnp.bfloat16)
    return stream


def solution(mesh):
    n_seq = mesh.shape["seq"]
    n_tp = mesh.shape["tp"]
    devices = np.asarray(mesh.devices).reshape(n_seq // 2, 2, n_tp)
    grid = Mesh(devices, ("zz", "core", "tp"))
    seq = ("zz", "core")
    in_specs = (
        P(seq, None, "tp"),
        P(seq, None),
        P(),
        P(None, ("zz", "core", "tp"), None),
        P(None, ("zz", "core", "tp"), None),
        P(None, "tp"),
        P(None, "tp"),
        P(None, "tp", None),
        P(None, "tp", None),
        P(None, "tp"),
        P(),
        P(),
    )
    out_specs = P(seq, None, "tp")
    return jax.shard_map(shards, mesh=grid, in_specs=in_specs, out_specs=out_specs, check_vma=False)
```

```python
import jax
import jax.numpy as jnp
import numpy as np
from jax import lax
from jax.sharding import Mesh
from jax.sharding import PartitionSpec as P

HD = 256
ROT = 64
LAYERS = 2
HEADS = 8


def layer_norm(values, gain, shift):
    mean = jnp.mean(values, axis=-1, keepdims=True)
    centred = values - mean
    var = jnp.mean(centred * centred, axis=-1, keepdims=True)
    return centred * lax.rsqrt(var + 1e-05) * gain + shift


def positions(segs):
    length = segs.shape[-1]
    index = jnp.broadcast_to(jnp.arange(length, dtype=jnp.int32), segs.shape)
    first = jnp.ones(segs.shape[:-1] + (1,), dtype=bool)
    flag = jnp.concatenate([first, segs[..., 1:] != segs[..., :-1]], axis=-1)
    start = lax.cummax(jnp.where(flag, index, 0), axis=segs.ndim - 1)
    return index - start


def rotate(values, pos):
    half = ROT // 2
    inverse = 10000.0 ** (-(jnp.arange(half, dtype=jnp.float32) * 2.0 / ROT))
    angle = pos[..., None].astype(jnp.float32) * inverse
    cosine = jnp.cos(angle)[..., None, :]
    sine = jnp.sin(angle)[..., None, :]
    first = values[..., :half]
    second = values[..., half:ROT]
    return jnp.concatenate(
        [first * cosine - second * sine, second * cosine + first * sine, values[..., ROT:]], axis=-1
    )


def attention(qkv, pos, mask):
    query = rotate(qkv[:, :, :, 0], pos).astype(jnp.bfloat16)
    keys = rotate(qkv[:, :, :, 1], pos).astype(jnp.bfloat16)
    vals = qkv[:, :, :, 2].astype(jnp.bfloat16)
    scores = jnp.einsum("rqhd,rkhd->rhqk", query, keys, preferred_element_type=jnp.float32) / jnp.sqrt(
        jnp.float32(HD)
    )
    scores = jnp.where(mask, scores, -jnp.inf)
    probs = jax.nn.softmax(scores, axis=-1).astype(jnp.bfloat16)
    ctx = jnp.einsum("rhqk,rkhd->rqhd", probs, vals, preferred_element_type=jnp.float32)
    return ctx.astype(jnp.bfloat16)


def shards(
    tokens,
    segment_ids,
    shard_map,
    trainer_qkv,
    trainer_up,
    qkv_bias,
    up_bias,
    dense_w,
    down_w,
    out_bias,
    norm_gain,
    norm_shift,
):
    n_zz = lax.axis_size("zz")
    n_core = lax.axis_size("core")
    n_tp = lax.axis_size("tp")
    core = lax.axis_index("core")
    _, length, _ = tokens.shape
    block = trainer_qkv.shape[1]
    full_width = trainer_qkv.shape[1] * n_zz * n_core * n_tp
    n_blocks = full_width // block
    heads_group = qkv_bias.shape[1] // (3 * HD)
    ff_group = up_bias.shape[1]
    ff_here = ff_group // n_core
    split_heads = heads_group % n_core == 0
    heads_here = heads_group // n_core if split_heads else heads_group
    qkv_cols = heads_here * 3 * HD
    n_dest = n_tp * n_core

    wq = trainer_qkv.astype(jnp.bfloat16)
    wu = trainer_up.astype(jnp.bfloat16)
    if split_heads:
        wq = wq.reshape(LAYERS, block, n_dest, qkv_cols)
    else:
        wq = wq.reshape(LAYERS, block, n_tp, 1, qkv_cols)
        wq = jnp.broadcast_to(wq, (LAYERS, block, n_tp, n_core, qkv_cols))
        wq = wq.reshape(LAYERS, block, n_dest, qkv_cols)
    wu = wu.reshape(LAYERS, block, n_dest, ff_here)
    packed = jnp.concatenate([wq, wu], axis=-1)
    packed = lax.all_to_all(packed, ("tp", "core"), split_axis=2, concat_axis=1, tiled=True)

    k_i, t_i, c_i = np.meshgrid(np.arange(n_zz), np.arange(n_tp), np.arange(n_core), indexing="ij")
    src_zz = (lax.axis_index("zz") + n_zz - jnp.asarray(k_i.reshape(-1), dtype=jnp.int32)) % n_zz
    source = (src_zz * n_core + jnp.asarray(c_i.reshape(-1))) * n_tp + jnp.asarray(t_i.reshape(-1))
    feature_block = jnp.take(shard_map, source.astype(jnp.int32))

    def gather_zz(piece):
        pieces = [piece]
        for k in range(1, n_zz):
            pieces.append(lax.ppermute(piece, "zz", perm=[(i, (i + k) % n_zz) for i in range(n_zz)]))
        return jnp.concatenate(pieces, axis=0)

    segs = lax.all_gather(segment_ids, "core", axis=0, tiled=True)
    rows = segs.shape[0]
    pos = positions(segs)
    index = jnp.arange(length, dtype=jnp.int32)
    mask = (index[None, :] <= index[:, None])[None] & (segs[:, :, None] == segs[:, None, :])
    mask = mask[:, None]
    bias_full = lax.all_gather(out_bias, "tp", axis=1, tiled=True)

    stream = lax.all_gather(tokens, "tp", axis=2, tiled=True)
    stream = lax.all_gather(stream, "core", axis=0, tiled=True)
    for layer in range(LAYERS):
        weights = gather_zz(packed[layer].reshape(n_dest * block, -1))
        w_qkv = weights[:, :qkv_cols]
        w_up = weights[:, qkv_cols:]
        flt = stream.astype(jnp.float32)
        permuted = jnp.take(stream.reshape(rows, length, n_blocks, block), feature_block, axis=2)
        permuted = permuted.reshape(rows * length, full_width).astype(jnp.float32)

        def norm_of(i):
            gain = jnp.take(norm_gain[layer, i].reshape(n_blocks, block), feature_block, axis=0)
            shift = jnp.take(norm_shift[layer, i].reshape(n_blocks, block), feature_block, axis=0)
            return layer_norm(permuted, gain.reshape(-1), shift.reshape(-1)).astype(jnp.bfloat16)

        attn_in = norm_of(0)
        mlp_in = norm_of(1)

        if split_heads:
            q_bias = lax.dynamic_slice_in_dim(qkv_bias[layer], core * qkv_cols, qkv_cols)
            qkv = jnp.dot(attn_in, w_qkv, preferred_element_type=jnp.float32) + q_bias.astype(jnp.float32)
            ctx = attention(qkv.reshape(rows, length, heads_here, 3, HD), pos, mask)
            ctx = ctx.reshape(rows * length, heads_here * HD)
            d_rows = lax.dynamic_slice_in_dim(dense_w[layer], core * heads_here * HD, heads_here * HD)
            attn_out = jnp.dot(ctx, d_rows, preferred_element_type=jnp.float32)
        else:
            own = lax.dynamic_slice_in_dim(attn_in.reshape(rows, length, -1), core, 1, axis=0)
            qkv = jnp.dot(own.reshape(length, -1), w_qkv, preferred_element_type=jnp.float32)
            qkv = qkv + qkv_bias[layer].astype(jnp.float32)
            own_pos = lax.dynamic_slice_in_dim(pos, core, 1, axis=0)
            own_mask = lax.dynamic_slice_in_dim(mask, core, 1, axis=0)
            ctx = attention(qkv.reshape(1, length, heads_here, 3, HD), own_pos, own_mask)
            attn_out = jnp.dot(ctx.reshape(length, -1), dense_w[layer], preferred_element_type=jnp.float32)
            here = (jnp.arange(rows) == core)[:, None, None]
            attn_out = jnp.where(here, attn_out[None], 0.0).reshape(rows * length, -1)

        u_bias = lax.dynamic_slice_in_dim(up_bias[layer], core * ff_here, ff_here)
        up = jnp.dot(mlp_in, w_up, preferred_element_type=jnp.float32) + u_bias.astype(jnp.float32)
        hidden_units = jax.nn.gelu(up, approximate=False).astype(jnp.bfloat16)
        m_rows = lax.dynamic_slice_in_dim(down_w[layer], core * ff_here, ff_here)
        partial_terms = attn_out + jnp.dot(hidden_units, m_rows, preferred_element_type=jnp.float32)
        partial_terms = partial_terms.astype(jnp.bfloat16).reshape(rows, length, full_width)
        if layer + 1 < LAYERS:
            summed = lax.psum(partial_terms, ("core", "tp")).astype(jnp.float32)
            stream = (flt + summed + bias_full[layer]).astype(jnp.bfloat16)
        else:
            summed = lax.psum_scatter(partial_terms, "core", scatter_dimension=0, tiled=True)
            summed = lax.psum_scatter(summed, "tp", scatter_dimension=2, tiled=True).astype(jnp.float32)
            width_here = full_width // n_tp
            own_stream = lax.dynamic_slice_in_dim(flt, core, 1, axis=0)
            own_stream = lax.dynamic_slice_in_dim(own_stream, lax.axis_index("tp") * width_here, width_here, axis=2)
            stream = (own_stream + summed + out_bias[layer]).astype(jnp.bfloat16)
    return stream


def solution(mesh):
    n_seq = mesh.shape["seq"]
    n_tp = mesh.shape["tp"]
    devices = np.asarray(mesh.devices).reshape(n_seq // 2, 2, n_tp)
    grid = Mesh(devices, ("zz", "core", "tp"))
    seq = ("zz", "core")
    in_specs = (
        P(seq, None, "tp"),
        P(seq, None),
        P(),
        P(None, ("zz", "core", "tp"), None),
        P(None, ("zz", "core", "tp"), None),
        P(None, "tp"),
        P(None, "tp"),
        P(None, "tp", None),
        P(None, "tp", None),
        P(None, "tp"),
        P(),
        P(),
    )
    out_specs = P(seq, None, "tp")
    return jax.shard_map(shards, mesh=grid, in_specs=in_specs, out_specs=out_specs, check_vma=False)
```

```python
import jax
import jax.numpy as jnp
import numpy as np
from jax import lax
from jax.sharding import Mesh
from jax.sharding import PartitionSpec as P

HD = 256
ROT = 64
LAYERS = 2
HEADS = 8


def layer_norm(values, gain, shift):
    mean = jnp.mean(values, axis=-1, keepdims=True)
    centred = values - mean
    var = jnp.mean(centred * centred, axis=-1, keepdims=True)
    return centred * lax.rsqrt(var + 1e-05) * gain + shift


def positions(segs):
    length = segs.shape[-1]
    index = jnp.broadcast_to(jnp.arange(length, dtype=jnp.int32), segs.shape)
    first = jnp.ones(segs.shape[:-1] + (1,), dtype=bool)
    flag = jnp.concatenate([first, segs[..., 1:] != segs[..., :-1]], axis=-1)
    start = lax.cummax(jnp.where(flag, index, 0), axis=segs.ndim - 1)
    return index - start


def rotate(values, pos):
    half = ROT // 2
    inverse = 10000.0 ** (-(jnp.arange(half, dtype=jnp.float32) * 2.0 / ROT))
    angle = pos[..., None].astype(jnp.float32) * inverse
    cosine = jnp.cos(angle)[..., None, :]
    sine = jnp.sin(angle)[..., None, :]
    first = values[..., :half]
    second = values[..., half:ROT]
    return jnp.concatenate(
        [first * cosine - second * sine, second * cosine + first * sine, values[..., ROT:]], axis=-1
    )


def attention(qkv, pos, mask):
    query = rotate(qkv[:, :, :, 0], pos).astype(jnp.bfloat16)
    keys = rotate(qkv[:, :, :, 1], pos).astype(jnp.bfloat16)
    vals = qkv[:, :, :, 2].astype(jnp.bfloat16)
    scores = jnp.einsum("rqhd,rkhd->rhqk", query, keys, preferred_element_type=jnp.float32) / jnp.sqrt(
        jnp.float32(HD)
    )
    scores = jnp.where(mask, scores, -jnp.inf)
    probs = jax.nn.softmax(scores, axis=-1).astype(jnp.bfloat16)
    ctx = jnp.einsum("rhqk,rkhd->rqhd", probs, vals, preferred_element_type=jnp.float32)
    return ctx.astype(jnp.bfloat16)


def shards(
    tokens,
    segment_ids,
    shard_map,
    trainer_qkv,
    trainer_up,
    qkv_bias,
    up_bias,
    dense_w,
    down_w,
    out_bias,
    norm_gain,
    norm_shift,
):
    n_zz = lax.axis_size("zz")
    n_core = lax.axis_size("core")
    n_tp = lax.axis_size("tp")
    core = lax.axis_index("core")
    _, length, _ = tokens.shape
    block = trainer_qkv.shape[1]
    full_width = trainer_qkv.shape[1] * n_zz * n_core * n_tp
    n_blocks = full_width // block
    heads_group = qkv_bias.shape[1] // (3 * HD)
    ff_group = up_bias.shape[1]
    ff_here = ff_group // n_core
    split_heads = heads_group % n_core == 0
    heads_here = heads_group // n_core if split_heads else heads_group
    qkv_cols = heads_here * 3 * HD
    n_dest = n_tp * n_core

    wq = trainer_qkv.astype(jnp.bfloat16)
    wu = trainer_up.astype(jnp.bfloat16)
    if split_heads:
        wq = wq.reshape(LAYERS, block, n_dest, qkv_cols)
    else:
        wq = wq.reshape(LAYERS, block, n_tp, 1, qkv_cols)
        wq = jnp.broadcast_to(wq, (LAYERS, block, n_tp, n_core, qkv_cols))
        wq = wq.reshape(LAYERS, block, n_dest, qkv_cols)
    wu = wu.reshape(LAYERS, block, n_dest, ff_here)
    packed = jnp.concatenate([wq, wu], axis=-1)
    packed = lax.all_to_all(packed, ("tp", "core"), split_axis=2, concat_axis=1, tiled=True)

    k_i, t_i, c_i = np.meshgrid(np.arange(n_zz), np.arange(n_tp), np.arange(n_core), indexing="ij")
    src_zz = (lax.axis_index("zz") + n_zz - jnp.asarray(k_i.reshape(-1), dtype=jnp.int32)) % n_zz
    source = (src_zz * n_core + jnp.asarray(c_i.reshape(-1))) * n_tp + jnp.asarray(t_i.reshape(-1))
    feature_block = jnp.take(shard_map, source.astype(jnp.int32))

    def gather_zz(piece):
        pieces = [piece]
        for k in range(1, n_zz):
            pieces.append(lax.ppermute(piece, "zz", perm=[(i, (i + k) % n_zz) for i in range(n_zz)]))
        return jnp.concatenate(pieces, axis=0)

    n_plane = n_core * n_tp
    me_plane = core * n_tp + lax.axis_index("tp")
    shifts = range(1, n_plane)

    def plane_perm(piece, k):
        return lax.ppermute(piece, ("core", "tp"), perm=[(i, (i + k) % n_plane) for i in range(n_plane)])

    def gather_plane(piece):
        width = piece.shape[2]
        whole = jnp.zeros((n_core, length, n_tp * width), piece.dtype)
        whole = lax.dynamic_update_slice(whole, piece, (core, 0, lax.axis_index("tp") * width))
        for k in shifts:
            src = (me_plane + n_plane - k) % n_plane
            got = plane_perm(piece, k)
            whole = lax.dynamic_update_slice(whole, got, (src // n_tp, 0, src % n_tp * width))
        return whole

    def scatter_plane(terms):
        width = terms.shape[2] // n_tp
        def block_of(dest):
            return lax.dynamic_slice(terms, (dest // n_tp, 0, dest % n_tp * width), (1, length, width))
        total = block_of(me_plane).astype(jnp.float32)
        for k in shifts:
            dest = (me_plane + k) % n_plane
            total = total + plane_perm(block_of(dest), k).astype(jnp.float32)
        return total

    segs = gather_plane(segment_ids[:, :, None])[:, :, 0::1].reshape(n_core, length * n_tp)
    segs = segs.reshape(n_core, length, n_tp)[:, :, 0]
    rows = n_core
    pos = positions(segs)
    index = jnp.arange(length, dtype=jnp.int32)
    mask = (index[None, :] <= index[:, None])[None] & (segs[:, :, None] == segs[:, None, :])
    mask = mask[:, None]

    local = tokens
    for layer in range(LAYERS):
        stream = gather_plane(local)
        weights = gather_zz(packed[layer].reshape(n_dest * block, -1))
        w_qkv = weights[:, :qkv_cols]
        w_up = weights[:, qkv_cols:]
        permuted = jnp.take(stream.reshape(rows, length, n_blocks, block), feature_block, axis=2)
        permuted = permuted.reshape(rows * length, full_width).astype(jnp.float32)

        def norm_of(i):
            gain = jnp.take(norm_gain[layer, i].reshape(n_blocks, block), feature_block, axis=0)
            shift = jnp.take(norm_shift[layer, i].reshape(n_blocks, block), feature_block, axis=0)
            return layer_norm(permuted, gain.reshape(-1), shift.reshape(-1)).astype(jnp.bfloat16)

        attn_in = norm_of(0)
        mlp_in = norm_of(1)

        if split_heads:
            q_bias = lax.dynamic_slice_in_dim(qkv_bias[layer], core * qkv_cols, qkv_cols)
            qkv = jnp.dot(attn_in, w_qkv, preferred_element_type=jnp.float32) + q_bias.astype(jnp.float32)
            ctx = attention(qkv.reshape(rows, length, heads_here, 3, HD), pos, mask)
            ctx = ctx.reshape(rows * length, heads_here * HD)
            d_rows = lax.dynamic_slice_in_dim(dense_w[layer], core * heads_here * HD, heads_here * HD)
            attn_out = jnp.dot(ctx, d_rows, preferred_element_type=jnp.float32)
        else:
            own = lax.dynamic_slice_in_dim(attn_in.reshape(rows, length, -1), core, 1, axis=0)
            qkv = jnp.dot(own.reshape(length, -1), w_qkv, preferred_element_type=jnp.float32)
            qkv = qkv + qkv_bias[layer].astype(jnp.float32)
            own_pos = lax.dynamic_slice_in_dim(pos, core, 1, axis=0)
            own_mask = lax.dynamic_slice_in_dim(mask, core, 1, axis=0)
            ctx = attention(qkv.reshape(1, length, heads_here, 3, HD), own_pos, own_mask)
            attn_out = jnp.dot(ctx.reshape(length, -1), dense_w[layer], preferred_element_type=jnp.float32)
            here = (jnp.arange(rows) == core)[:, None, None]
            attn_out = jnp.where(here, attn_out[None], 0.0).reshape(rows * length, -1)

        u_bias = lax.dynamic_slice_in_dim(up_bias[layer], core * ff_here, ff_here)
        up = jnp.dot(mlp_in, w_up, preferred_element_type=jnp.float32) + u_bias.astype(jnp.float32)
        hidden_units = jax.nn.gelu(up, approximate=False).astype(jnp.bfloat16)
        m_rows = lax.dynamic_slice_in_dim(down_w[layer], core * ff_here, ff_here)
        partial_terms = attn_out + jnp.dot(hidden_units, m_rows, preferred_element_type=jnp.float32)
        partial_terms = partial_terms.astype(jnp.bfloat16).reshape(rows, length, full_width)
        summed = scatter_plane(partial_terms)
        local = (local.astype(jnp.float32) + summed + out_bias[layer]).astype(jnp.bfloat16)
    stream = local
    return stream


def solution(mesh):
    n_seq = mesh.shape["seq"]
    n_tp = mesh.shape["tp"]
    devices = np.asarray(mesh.devices).reshape(n_seq // 2, 2, n_tp)
    grid = Mesh(devices, ("zz", "core", "tp"))
    seq = ("zz", "core")
    in_specs = (
        P(seq, None, "tp"),
        P(seq, None),
        P(),
        P(None, ("zz", "core", "tp"), None),
        P(None, ("zz", "core", "tp"), None),
        P(None, "tp"),
        P(None, "tp"),
        P(None, "tp", None),
        P(None, "tp", None),
        P(None, "tp"),
        P(),
        P(),
    )
    out_specs = P(seq, None, "tp")
    return jax.shard_map(shards, mesh=grid, in_specs=in_specs, out_specs=out_specs, check_vma=False)
```

```python
import jax
import jax.numpy as jnp
import numpy as np
from jax import lax
from jax.sharding import Mesh
from jax.sharding import PartitionSpec as P

HD = 256
ROT = 64
LAYERS = 2
HEADS = 8


def layer_norm(values, gain, shift):
    mean = jnp.mean(values, axis=-1, keepdims=True)
    centred = values - mean
    var = jnp.mean(centred * centred, axis=-1, keepdims=True)
    return centred * lax.rsqrt(var + 1e-05) * gain + shift


def positions(segs):
    length = segs.shape[-1]
    index = jnp.broadcast_to(jnp.arange(length, dtype=jnp.int32), segs.shape)
    first = jnp.ones(segs.shape[:-1] + (1,), dtype=bool)
    flag = jnp.concatenate([first, segs[..., 1:] != segs[..., :-1]], axis=-1)
    start = lax.cummax(jnp.where(flag, index, 0), axis=segs.ndim - 1)
    return index - start


def rotate(values, pos):
    half = ROT // 2
    inverse = 10000.0 ** (-(jnp.arange(half, dtype=jnp.float32) * 2.0 / ROT))
    angle = pos[..., None].astype(jnp.float32) * inverse
    cosine = jnp.cos(angle)[..., None, :]
    sine = jnp.sin(angle)[..., None, :]
    first = values[..., :half]
    second = values[..., half:ROT]
    return jnp.concatenate(
        [first * cosine - second * sine, second * cosine + first * sine, values[..., ROT:]], axis=-1
    )


def attention(qkv, pos, mask):
    query = rotate(qkv[:, :, :, 0], pos).astype(jnp.bfloat16)
    keys = rotate(qkv[:, :, :, 1], pos).astype(jnp.bfloat16)
    vals = qkv[:, :, :, 2].astype(jnp.bfloat16)
    scores = jnp.einsum("rqhd,rkhd->rhqk", query, keys, preferred_element_type=jnp.float32) / jnp.sqrt(
        jnp.float32(HD)
    )
    scores = jnp.where(mask, scores, -jnp.inf)
    probs = jax.nn.softmax(scores, axis=-1).astype(jnp.bfloat16)
    ctx = jnp.einsum("rhqk,rkhd->rqhd", probs, vals, preferred_element_type=jnp.float32)
    return ctx.astype(jnp.bfloat16)


def shards(
    tokens,
    segment_ids,
    shard_map,
    trainer_qkv,
    trainer_up,
    qkv_bias,
    up_bias,
    dense_w,
    down_w,
    out_bias,
    norm_gain,
    norm_shift,
):
    n_zz = lax.axis_size("zz")
    n_core = lax.axis_size("core")
    n_tp = lax.axis_size("tp")
    core = lax.axis_index("core")
    _, length, _ = tokens.shape
    block = trainer_qkv.shape[1]
    full_width = trainer_qkv.shape[1] * n_zz * n_core * n_tp
    n_blocks = full_width // block
    heads_group = qkv_bias.shape[1] // (3 * HD)
    ff_group = up_bias.shape[1]
    ff_here = ff_group // n_core
    split_heads = heads_group % n_core == 0
    heads_here = heads_group // n_core if split_heads else heads_group
    qkv_cols = heads_here * 3 * HD
    n_dest = n_tp * n_core

    wq = trainer_qkv.astype(jnp.bfloat16)
    wu = trainer_up.astype(jnp.bfloat16)
    if split_heads:
        wq = wq.reshape(LAYERS, block, n_dest, qkv_cols)
    else:
        wq = wq.reshape(LAYERS, block, n_tp, 1, qkv_cols)
        wq = jnp.broadcast_to(wq, (LAYERS, block, n_tp, n_core, qkv_cols))
        wq = wq.reshape(LAYERS, block, n_dest, qkv_cols)
    wu = wu.reshape(LAYERS, block, n_dest, ff_here)
    packed = jnp.concatenate([wq, wu], axis=-1)
    packed = lax.all_to_all(packed, ("tp", "core"), split_axis=2, concat_axis=1, tiled=True)

    k_i, t_i, c_i = np.meshgrid(np.arange(n_zz), np.arange(n_tp), np.arange(n_core), indexing="ij")
    src_zz = (lax.axis_index("zz") + n_zz - jnp.asarray(k_i.reshape(-1), dtype=jnp.int32)) % n_zz
    source = (src_zz * n_core + jnp.asarray(c_i.reshape(-1))) * n_tp + jnp.asarray(t_i.reshape(-1))
    feature_block = jnp.take(shard_map, source.astype(jnp.int32))

    def gather_zz(piece):
        pieces = [piece]
        for k in range(1, n_zz):
            pieces.append(lax.ppermute(piece, "zz", perm=[(i, (i + k) % n_zz) for i in range(n_zz)]))
        return jnp.concatenate(pieces, axis=0)

    n_plane = n_core * n_tp
    plane = ("core", "tp")

    def gather_plane(piece):
        width = piece.shape[2]
        spread = jnp.broadcast_to(piece, (n_plane, length, width))
        got = lax.all_to_all(spread, plane, split_axis=0, concat_axis=0, tiled=True)
        got = got.reshape(n_core, n_tp, length, width).transpose(0, 2, 1, 3)
        return got.reshape(n_core, length, n_tp * width)

    def scatter_plane(terms):
        width = terms.shape[2] // n_tp
        terms = terms.reshape(n_core, length, n_tp, width).transpose(0, 2, 1, 3)
        terms = terms.reshape(n_plane, length, width)
        got = lax.all_to_all(terms, plane, split_axis=0, concat_axis=0, tiled=True)
        return jnp.sum(got.astype(jnp.float32), axis=0, keepdims=True)

    other = lax.ppermute(segment_ids, "core", perm=[(i, (i + 1) % n_core) for i in range(n_core)])
    segs = jnp.where(core == 0, jnp.concatenate([segment_ids, other]), jnp.concatenate([other, segment_ids]))
    rows = n_core
    pos = positions(segs)
    index = jnp.arange(length, dtype=jnp.int32)
    mask = (index[None, :] <= index[:, None])[None] & (segs[:, :, None] == segs[:, None, :])
    mask = mask[:, None]

    local = tokens
    for layer in range(LAYERS):
        stream = gather_plane(local)
        weights = gather_zz(packed[layer].reshape(n_dest * block, -1))
        w_qkv = weights[:, :qkv_cols]
        w_up = weights[:, qkv_cols:]
        permuted = jnp.take(stream.reshape(rows, length, n_blocks, block), feature_block, axis=2)
        permuted = permuted.reshape(rows * length, full_width).astype(jnp.float32)

        def norm_of(i):
            gain = jnp.take(norm_gain[layer, i].reshape(n_blocks, block), feature_block, axis=0)
            shift = jnp.take(norm_shift[layer, i].reshape(n_blocks, block), feature_block, axis=0)
            return layer_norm(permuted, gain.reshape(-1), shift.reshape(-1)).astype(jnp.bfloat16)

        attn_in = norm_of(0)
        mlp_in = norm_of(1)

        if split_heads:
            q_bias = lax.dynamic_slice_in_dim(qkv_bias[layer], core * qkv_cols, qkv_cols)
            qkv = jnp.dot(attn_in, w_qkv, preferred_element_type=jnp.float32) + q_bias.astype(jnp.float32)
            ctx = attention(qkv.reshape(rows, length, heads_here, 3, HD), pos, mask)
            ctx = ctx.reshape(rows * length, heads_here * HD)
            d_rows = lax.dynamic_slice_in_dim(dense_w[layer], core * heads_here * HD, heads_here * HD)
            attn_out = jnp.dot(ctx, d_rows, preferred_element_type=jnp.float32)
        else:
            own = lax.dynamic_slice_in_dim(attn_in.reshape(rows, length, -1), core, 1, axis=0)
            qkv = jnp.dot(own.reshape(length, -1), w_qkv, preferred_element_type=jnp.float32)
            qkv = qkv + qkv_bias[layer].astype(jnp.float32)
            own_pos = lax.dynamic_slice_in_dim(pos, core, 1, axis=0)
            own_mask = lax.dynamic_slice_in_dim(mask, core, 1, axis=0)
            ctx = attention(qkv.reshape(1, length, heads_here, 3, HD), own_pos, own_mask)
            attn_out = jnp.dot(ctx.reshape(length, -1), dense_w[layer], preferred_element_type=jnp.float32)
            here = (jnp.arange(rows) == core)[:, None, None]
            attn_out = jnp.where(here, attn_out[None], 0.0).reshape(rows * length, -1)

        u_bias = lax.dynamic_slice_in_dim(up_bias[layer], core * ff_here, ff_here)
        up = jnp.dot(mlp_in, w_up, preferred_element_type=jnp.float32) + u_bias.astype(jnp.float32)
        hidden_units = jax.nn.gelu(up, approximate=False).astype(jnp.bfloat16)
        m_rows = lax.dynamic_slice_in_dim(down_w[layer], core * ff_here, ff_here)
        partial_terms = attn_out + jnp.dot(hidden_units, m_rows, preferred_element_type=jnp.float32)
        partial_terms = partial_terms.astype(jnp.bfloat16).reshape(rows, length, full_width)
        summed = scatter_plane(partial_terms)
        local = (local.astype(jnp.float32) + summed + out_bias[layer]).astype(jnp.bfloat16)
    stream = local
    return stream


def solution(mesh):
    n_seq = mesh.shape["seq"]
    n_tp = mesh.shape["tp"]
    devices = np.asarray(mesh.devices).reshape(n_seq // 2, 2, n_tp)
    grid = Mesh(devices, ("zz", "core", "tp"))
    seq = ("zz", "core")
    in_specs = (
        P(seq, None, "tp"),
        P(seq, None),
        P(),
        P(None, ("zz", "core", "tp"), None),
        P(None, ("zz", "core", "tp"), None),
        P(None, "tp"),
        P(None, "tp"),
        P(None, "tp", None),
        P(None, "tp", None),
        P(None, "tp"),
        P(),
        P(),
    )
    out_specs = P(seq, None, "tp")
    return jax.shard_map(shards, mesh=grid, in_specs=in_specs, out_specs=out_specs, check_vma=False)
```

```python
import jax
import jax.numpy as jnp
import numpy as np
from jax import lax
from jax.sharding import Mesh
from jax.sharding import PartitionSpec as P

HD = 256
ROT = 64
LAYERS = 2
HEADS = 8


def layer_norm(values, gain, shift):
    mean = jnp.mean(values, axis=-1, keepdims=True)
    centred = values - mean
    var = jnp.mean(centred * centred, axis=-1, keepdims=True)
    return centred * lax.rsqrt(var + 1e-05) * gain + shift


def positions(segs):
    length = segs.shape[-1]
    index = jnp.broadcast_to(jnp.arange(length, dtype=jnp.int32), segs.shape)
    first = jnp.ones(segs.shape[:-1] + (1,), dtype=bool)
    flag = jnp.concatenate([first, segs[..., 1:] != segs[..., :-1]], axis=-1)
    start = lax.cummax(jnp.where(flag, index, 0), axis=segs.ndim - 1)
    return index - start


def rotate(values, pos):
    half = ROT // 2
    inverse = 10000.0 ** (-(jnp.arange(half, dtype=jnp.float32) * 2.0 / ROT))
    angle = pos[..., None].astype(jnp.float32) * inverse
    cosine = jnp.cos(angle)[..., None, :]
    sine = jnp.sin(angle)[..., None, :]
    first = values[..., :half]
    second = values[..., half:ROT]
    return jnp.concatenate(
        [first * cosine - second * sine, second * cosine + first * sine, values[..., ROT:]], axis=-1
    )


def attention(qkv, pos, mask):
    query = rotate(qkv[:, :, :, 0], pos).astype(jnp.bfloat16)
    keys = rotate(qkv[:, :, :, 1], pos).astype(jnp.bfloat16)
    vals = qkv[:, :, :, 2].astype(jnp.bfloat16)
    scores = jnp.einsum("rqhd,rkhd->rhqk", query, keys, preferred_element_type=jnp.float32) / jnp.sqrt(
        jnp.float32(HD)
    )
    scores = jnp.where(mask, scores, -jnp.inf)
    probs = jax.nn.softmax(scores, axis=-1).astype(jnp.bfloat16)
    ctx = jnp.einsum("rhqk,rkhd->rqhd", probs, vals, preferred_element_type=jnp.float32)
    return ctx.astype(jnp.bfloat16)


def shards(
    tokens,
    segment_ids,
    shard_map,
    trainer_qkv,
    trainer_up,
    qkv_bias,
    up_bias,
    dense_w,
    down_w,
    out_bias,
    norm_gain,
    norm_shift,
):
    n_zz = lax.axis_size("zz")
    n_core = lax.axis_size("core")
    n_tp = lax.axis_size("tp")
    core = lax.axis_index("core")
    _, length, _ = tokens.shape
    block = trainer_qkv.shape[1]
    full_width = trainer_qkv.shape[1] * n_zz * n_core * n_tp
    n_blocks = full_width // block
    heads_group = qkv_bias.shape[1] // (3 * HD)
    ff_group = up_bias.shape[1]
    ff_here = ff_group // n_core
    split_heads = heads_group % n_core == 0
    heads_here = heads_group // n_core if split_heads else heads_group
    qkv_cols = heads_here * 3 * HD
    n_dest = n_tp * n_core

    wq = trainer_qkv.astype(jnp.bfloat16)
    wu = trainer_up.astype(jnp.bfloat16)
    if split_heads:
        wq = wq.reshape(LAYERS, block, n_dest, qkv_cols)
    else:
        wq = wq.reshape(LAYERS, block, n_tp, 1, qkv_cols)
        wq = jnp.broadcast_to(wq, (LAYERS, block, n_tp, n_core, qkv_cols))
        wq = wq.reshape(LAYERS, block, n_dest, qkv_cols)
    wu = wu.reshape(LAYERS, block, n_dest, ff_here)
    packed = jnp.concatenate([wq, wu], axis=-1)
    packed = lax.all_to_all(packed, ("tp", "core"), split_axis=2, concat_axis=1, tiled=True)

    k_i, t_i, c_i = np.meshgrid(np.arange(n_zz), np.arange(n_tp), np.arange(n_core), indexing="ij")
    src_zz = (lax.axis_index("zz") + n_zz - jnp.asarray(k_i.reshape(-1), dtype=jnp.int32)) % n_zz
    source = (src_zz * n_core + jnp.asarray(c_i.reshape(-1))) * n_tp + jnp.asarray(t_i.reshape(-1))
    feature_block = jnp.take(shard_map, source.astype(jnp.int32))

    def gather_zz(piece):
        pieces = [piece]
        for k in range(1, n_zz):
            pieces.append(lax.ppermute(piece, "zz", perm=[(i, (i + k) % n_zz) for i in range(n_zz)]))
        return jnp.concatenate(pieces, axis=0)

    n_plane = n_core * n_tp
    plane = ("core", "tp")

    def gather_plane(piece):
        width = piece.shape[2]
        spread = jnp.broadcast_to(piece, (n_plane, length, width))
        got = lax.all_to_all(spread, plane, split_axis=0, concat_axis=0, tiled=True)
        got = got.reshape(n_core, n_tp, length, width).transpose(0, 2, 1, 3)
        return got.reshape(n_core, length, n_tp * width)

    def scatter_plane(terms):
        width = terms.shape[2] // n_tp
        terms = terms.reshape(n_core, length, n_tp, width).transpose(0, 2, 1, 3)
        terms = terms.reshape(n_plane, length, width)
        got = lax.all_to_all(terms, plane, split_axis=0, concat_axis=0, tiled=True)
        return jnp.sum(got.astype(jnp.float32), axis=0, keepdims=True)

    other = lax.ppermute(segment_ids, "core", perm=[(i, (i + 1) % n_core) for i in range(n_core)])
    segs = jnp.where(core == 0, jnp.concatenate([segment_ids, other]), jnp.concatenate([other, segment_ids]))
    rows = n_core
    pos = positions(segs)
    index = jnp.arange(length, dtype=jnp.int32)
    mask = (index[None, :] <= index[:, None])[None] & (segs[:, :, None] == segs[:, None, :])
    mask = mask[:, None]

    gathered = [gather_zz(packed[0].reshape(n_dest * block, -1))]
    for layer in range(1, LAYERS):
        piece, gathered[-1] = lax.optimization_barrier((packed[layer], gathered[-1]))
        gathered.append(gather_zz(piece.reshape(n_dest * block, -1)))

    local = tokens
    for layer in range(LAYERS):
        stream = gather_plane(local)
        weights = gathered[layer]
        w_qkv = weights[:, :qkv_cols]
        w_up = weights[:, qkv_cols:]
        permuted = jnp.take(stream.reshape(rows, length, n_blocks, block), feature_block, axis=2)
        permuted = permuted.reshape(rows * length, full_width).astype(jnp.float32)

        def norm_of(i):
            gain = jnp.take(norm_gain[layer, i].reshape(n_blocks, block), feature_block, axis=0)
            shift = jnp.take(norm_shift[layer, i].reshape(n_blocks, block), feature_block, axis=0)
            return layer_norm(permuted, gain.reshape(-1), shift.reshape(-1)).astype(jnp.bfloat16)

        attn_in = norm_of(0)
        mlp_in = norm_of(1)

        if split_heads:
            q_bias = lax.dynamic_slice_in_dim(qkv_bias[layer], core * qkv_cols, qkv_cols)
            qkv = jnp.dot(attn_in, w_qkv, preferred_element_type=jnp.float32) + q_bias.astype(jnp.float32)
            ctx = attention(qkv.reshape(rows, length, heads_here, 3, HD), pos, mask)
            ctx = ctx.reshape(rows * length, heads_here * HD)
            d_rows = lax.dynamic_slice_in_dim(dense_w[layer], core * heads_here * HD, heads_here * HD)
            attn_out = jnp.dot(ctx, d_rows, preferred_element_type=jnp.float32)
        else:
            own = lax.dynamic_slice_in_dim(attn_in.reshape(rows, length, -1), core, 1, axis=0)
            qkv = jnp.dot(own.reshape(length, -1), w_qkv, preferred_element_type=jnp.float32)
            qkv = qkv + qkv_bias[layer].astype(jnp.float32)
            own_pos = lax.dynamic_slice_in_dim(pos, core, 1, axis=0)
            own_mask = lax.dynamic_slice_in_dim(mask, core, 1, axis=0)
            ctx = attention(qkv.reshape(1, length, heads_here, 3, HD), own_pos, own_mask)
            attn_out = jnp.dot(ctx.reshape(length, -1), dense_w[layer], preferred_element_type=jnp.float32)
            here = (jnp.arange(rows) == core)[:, None, None]
            attn_out = jnp.where(here, attn_out[None], 0.0).reshape(rows * length, -1)

        u_bias = lax.dynamic_slice_in_dim(up_bias[layer], core * ff_here, ff_here)
        up = jnp.dot(mlp_in, w_up, preferred_element_type=jnp.float32) + u_bias.astype(jnp.float32)
        hidden_units = jax.nn.gelu(up, approximate=False).astype(jnp.bfloat16)
        m_rows = lax.dynamic_slice_in_dim(down_w[layer], core * ff_here, ff_here)
        partial_terms = attn_out + jnp.dot(hidden_units, m_rows, preferred_element_type=jnp.float32)
        partial_terms = partial_terms.astype(jnp.bfloat16).reshape(rows, length, full_width)
        if layer + 1 < LAYERS:
            partial_terms, gathered[layer + 1] = lax.optimization_barrier((partial_terms, gathered[layer + 1]))
        summed = scatter_plane(partial_terms)
        local = (local.astype(jnp.float32) + summed + out_bias[layer]).astype(jnp.bfloat16)
    stream = local
    return stream


def solution(mesh):
    n_seq = mesh.shape["seq"]
    n_tp = mesh.shape["tp"]
    devices = np.asarray(mesh.devices).reshape(n_seq // 2, 2, n_tp)
    grid = Mesh(devices, ("zz", "core", "tp"))
    seq = ("zz", "core")
    in_specs = (
        P(seq, None, "tp"),
        P(seq, None),
        P(),
        P(None, ("zz", "core", "tp"), None),
        P(None, ("zz", "core", "tp"), None),
        P(None, "tp"),
        P(None, "tp"),
        P(None, "tp", None),
        P(None, "tp", None),
        P(None, "tp"),
        P(),
        P(),
    )
    out_specs = P(seq, None, "tp")
    return jax.shard_map(shards, mesh=grid, in_specs=in_specs, out_specs=out_specs, check_vma=False)
```

```python
import jax
import jax.numpy as jnp
from jax import lax
from jax.sharding import PartitionSpec as P

HD = 256
ROT = 64
LAYERS = 2


def layer_norm(values, gain, shift):
    mean = jnp.mean(values, axis=-1, keepdims=True)
    centred = values - mean
    var = jnp.mean(centred * centred, axis=-1, keepdims=True)
    return centred * lax.rsqrt(var + 1e-05) * gain + shift


def positions(segs):
    length = segs.shape[-1]
    index = jnp.broadcast_to(jnp.arange(length, dtype=jnp.int32), segs.shape)
    first = jnp.ones(segs.shape[:-1] + (1,), dtype=bool)
    flag = jnp.concatenate([first, segs[..., 1:] != segs[..., :-1]], axis=-1)
    start = lax.cummax(jnp.where(flag, index, 0), axis=segs.ndim - 1)
    return index - start


def rotate(values, pos):
    half = ROT // 2
    inverse = 10000.0 ** (-(jnp.arange(half, dtype=jnp.float32) * 2.0 / ROT))
    angle = pos[..., None].astype(jnp.float32) * inverse
    cosine = jnp.cos(angle)[..., None, :]
    sine = jnp.sin(angle)[..., None, :]
    first = values[..., :half]
    second = values[..., half:ROT]
    return jnp.concatenate(
        [first * cosine - second * sine, second * cosine + first * sine, values[..., ROT:]], axis=-1
    )


def shards(
    tokens,
    segment_ids,
    shard_map,
    trainer_qkv,
    trainer_up,
    qkv_bias,
    up_bias,
    dense_w,
    down_w,
    out_bias,
    norm_gain,
    norm_shift,
):
    n_tp = lax.axis_size("tp")
    rows, length, _ = tokens.shape
    block = trainer_qkv.shape[1]
    full_width = block * n_tp * lax.axis_size("seq")
    n_blocks = full_width // block
    heads_here = qkv_bias.shape[1] // (3 * HD)
    qkv_cols = qkv_bias.shape[1]

    wq = trainer_qkv.astype(jnp.bfloat16).reshape(LAYERS, block, n_tp, qkv_cols)
    wu = trainer_up.astype(jnp.bfloat16).reshape(LAYERS, block, n_tp, up_bias.shape[1])
    packed = jnp.concatenate([wq, wu], axis=-1)
    packed = lax.all_to_all(packed, "tp", split_axis=2, concat_axis=1, tiled=True)
    gathered = [lax.all_gather(packed[layer].reshape(n_tp * block, -1), "seq", axis=0, tiled=True) for layer in range(LAYERS)]

    pos = positions(segment_ids)
    index = jnp.arange(length, dtype=jnp.int32)
    mask = (index[None, :] <= index[:, None])[None] & (
        segment_ids[:, :, None] == segment_ids[:, None, :]
    )
    mask = mask[:, None]
    stream = tokens
    for layer in range(LAYERS):
        weights = gathered[layer]
        qkv_mat = weights[:, :qkv_cols]
        up_mat = weights[:, qkv_cols:]
        whole = lax.all_gather(stream, "tp", axis=2, tiled=True)
        permuted = jnp.take(whole.reshape(rows, length, n_blocks, block), shard_map, axis=2)
        permuted = permuted.reshape(rows * length, full_width).astype(jnp.float32)

        def norm_of(i):
            gain = jnp.take(norm_gain[layer, i].reshape(n_blocks, block), shard_map, axis=0)
            shift = jnp.take(norm_shift[layer, i].reshape(n_blocks, block), shard_map, axis=0)
            return layer_norm(permuted, gain.reshape(-1), shift.reshape(-1)).astype(jnp.bfloat16)

        attn_in = norm_of(0)
        mlp_in = norm_of(1)
        qkv = jnp.dot(attn_in, qkv_mat, preferred_element_type=jnp.float32) + qkv_bias[layer].astype(jnp.float32)
        qkv = qkv.reshape(rows, length, heads_here, 3, HD)
        query = rotate(qkv[:, :, :, 0], pos).astype(jnp.bfloat16)
        keys = rotate(qkv[:, :, :, 1], pos).astype(jnp.bfloat16)
        vals = qkv[:, :, :, 2].astype(jnp.bfloat16)
        scores = jnp.einsum(
            "rqhd,rkhd->rhqk", query, keys, preferred_element_type=jnp.float32
        ) / jnp.sqrt(jnp.float32(HD))
        scores = jnp.where(mask, scores, -jnp.inf)
        probs = jax.nn.softmax(scores, axis=-1).astype(jnp.bfloat16)
        ctx = jnp.einsum("rhqk,rkhd->rqhd", probs, vals, preferred_element_type=jnp.float32).astype(
            jnp.bfloat16
        )
        ctx = ctx.reshape(rows * length, heads_here * HD)
        up = jnp.dot(mlp_in, up_mat, preferred_element_type=jnp.float32) + up_bias[layer].astype(jnp.float32)
        hidden_units = jax.nn.gelu(up, approximate=False).astype(jnp.bfloat16)
        partial_terms = jnp.dot(ctx, dense_w[layer], preferred_element_type=jnp.float32) + jnp.dot(
            hidden_units, down_w[layer], preferred_element_type=jnp.float32
        )
        partial_terms = partial_terms.astype(jnp.bfloat16)
        if layer + 1 < LAYERS:
            partial_terms, gathered[layer + 1] = lax.optimization_barrier((partial_terms, gathered[layer + 1]))
        summed = lax.psum_scatter(partial_terms, "tp", scatter_dimension=1, tiled=True).astype(jnp.float32)
        flat_stream = stream.astype(jnp.float32).reshape(rows * length, -1)
        stream = (flat_stream + summed + out_bias[layer]).astype(jnp.bfloat16).reshape(rows, length, -1)
    return stream


def solution(mesh):
    in_specs = (
        P("seq", None, "tp"),
        P("seq", None),
        P(),
        P(None, ("seq", "tp"), None),
        P(None, ("seq", "tp"), None),
        P(None, "tp"),
        P(None, "tp"),
        P(None, "tp", None),
        P(None, "tp", None),
        P(None, "tp"),
        P(),
        P(),
    )
    out_specs = P("seq", None, "tp")
    return jax.shard_map(shards, mesh=mesh, in_specs=in_specs, out_specs=out_specs, check_vma=False)
```

```python
import jax
import jax.numpy as jnp
from jax import lax
from jax.sharding import PartitionSpec as P

HD = 256
ROT = 64
LAYERS = 2


def layer_norm(values, gain, shift):
    mean = jnp.mean(values, axis=-1, keepdims=True)
    centred = values - mean
    var = jnp.mean(centred * centred, axis=-1, keepdims=True)
    return centred * lax.rsqrt(var + 1e-05) * gain + shift


def positions(segs):
    length = segs.shape[-1]
    index = jnp.broadcast_to(jnp.arange(length, dtype=jnp.int32), segs.shape)
    first = jnp.ones(segs.shape[:-1] + (1,), dtype=bool)
    flag = jnp.concatenate([first, segs[..., 1:] != segs[..., :-1]], axis=-1)
    start = lax.cummax(jnp.where(flag, index, 0), axis=segs.ndim - 1)
    return index - start


def rotate(values, pos):
    half = ROT // 2
    inverse = 10000.0 ** (-(jnp.arange(half, dtype=jnp.float32) * 2.0 / ROT))
    angle = pos[..., None].astype(jnp.float32) * inverse
    cosine = jnp.cos(angle)[..., None, :]
    sine = jnp.sin(angle)[..., None, :]
    first = values[..., :half]
    second = values[..., half:ROT]
    return jnp.concatenate(
        [first * cosine - second * sine, second * cosine + first * sine, values[..., ROT:]], axis=-1
    )


def shards(
    tokens,
    segment_ids,
    shard_map,
    trainer_qkv,
    trainer_up,
    qkv_bias,
    up_bias,
    dense_w,
    down_w,
    out_bias,
    norm_gain,
    norm_shift,
):
    n_tp = lax.axis_size("tp")
    rows, length, _ = tokens.shape
    block = trainer_qkv.shape[1]
    full_width = block * n_tp * lax.axis_size("seq")
    n_blocks = full_width // block
    heads_here = qkv_bias.shape[1] // (3 * HD)
    qkv_cols = qkv_bias.shape[1]

    wq = trainer_qkv.astype(jnp.bfloat16).reshape(LAYERS, block, n_tp, qkv_cols)
    wu = trainer_up.astype(jnp.bfloat16).reshape(LAYERS, block, n_tp, up_bias.shape[1])
    packed = jnp.concatenate([wq, wu], axis=-1).transpose(0, 2, 1, 3).reshape(LAYERS, n_tp, -1)
    cols = packed.shape[2] // block
    width_here = tokens.shape[2]

    def exchange(x):
        return lax.all_to_all(x, "tp", split_axis=0, concat_axis=0, tiled=True)

    def spread(local):
        return jnp.broadcast_to(local.reshape(1, -1), (n_tp, local.size))

    def joined(got):
        got = got.reshape(n_tp, rows, length, width_here).transpose(1, 2, 0, 3)
        return got.reshape(rows, length, n_tp * width_here)

    first = exchange(jnp.concatenate([packed[0], spread(tokens)], axis=1))
    pieces = [first[:, : block * cols]] + [exchange(packed[layer]) for layer in range(1, LAYERS)]
    whole = joined(first[:, block * cols :])
    gathered = [lax.all_gather(piece.reshape(n_tp * block, cols), "seq", axis=0, tiled=True) for piece in pieces]

    pos = positions(segment_ids)
    index = jnp.arange(length, dtype=jnp.int32)
    mask = (index[None, :] <= index[:, None])[None] & (
        segment_ids[:, :, None] == segment_ids[:, None, :]
    )
    mask = mask[:, None]
    stream = tokens
    for layer in range(LAYERS):
        weights = gathered[layer]
        qkv_mat = weights[:, :qkv_cols]
        up_mat = weights[:, qkv_cols:]
        if layer > 0:
            whole = joined(exchange(spread(stream)))
        permuted = jnp.take(whole.reshape(rows, length, n_blocks, block), shard_map, axis=2)
        permuted = permuted.reshape(rows * length, full_width).astype(jnp.float32)

        def norm_of(i):
            gain = jnp.take(norm_gain[layer, i].reshape(n_blocks, block), shard_map, axis=0)
            shift = jnp.take(norm_shift[layer, i].reshape(n_blocks, block), shard_map, axis=0)
            return layer_norm(permuted, gain.reshape(-1), shift.reshape(-1)).astype(jnp.bfloat16)

        attn_in = norm_of(0)
        mlp_in = norm_of(1)
        qkv = jnp.dot(attn_in, qkv_mat, preferred_element_type=jnp.float32) + qkv_bias[layer].astype(jnp.float32)
        qkv = qkv.reshape(rows, length, heads_here, 3, HD)
        query = rotate(qkv[:, :, :, 0], pos).astype(jnp.bfloat16)
        keys = rotate(qkv[:, :, :, 1], pos).astype(jnp.bfloat16)
        vals = qkv[:, :, :, 2].astype(jnp.bfloat16)
        scores = jnp.einsum(
            "rqhd,rkhd->rhqk", query, keys, preferred_element_type=jnp.float32
        ) / jnp.sqrt(jnp.float32(HD))
        scores = jnp.where(mask, scores, -jnp.inf)
        probs = jax.nn.softmax(scores, axis=-1).astype(jnp.bfloat16)
        ctx = jnp.einsum("rhqk,rkhd->rqhd", probs, vals, preferred_element_type=jnp.float32).astype(
            jnp.bfloat16
        )
        ctx = ctx.reshape(rows * length, heads_here * HD)
        up = jnp.dot(mlp_in, up_mat, preferred_element_type=jnp.float32) + up_bias[layer].astype(jnp.float32)
        hidden_units = jax.nn.gelu(up, approximate=False).astype(jnp.bfloat16)
        partial_terms = jnp.dot(ctx, dense_w[layer], preferred_element_type=jnp.float32) + jnp.dot(
            hidden_units, down_w[layer], preferred_element_type=jnp.float32
        )
        partial_terms = partial_terms.astype(jnp.bfloat16)
        if layer + 1 < LAYERS:
            split = partial_terms.reshape(rows * length, n_tp, width_here).transpose(1, 0, 2)
            summed = jnp.sum(exchange(split).astype(jnp.float32), axis=0)
        else:
            summed = lax.psum_scatter(partial_terms, "tp", scatter_dimension=1, tiled=True).astype(jnp.float32)
        flat_stream = stream.astype(jnp.float32).reshape(rows * length, -1)
        stream = (flat_stream + summed + out_bias[layer]).astype(jnp.bfloat16).reshape(rows, length, -1)
    return stream


def solution(mesh):
    in_specs = (
        P("seq", None, "tp"),
        P("seq", None),
        P(),
        P(None, ("seq", "tp"), None),
        P(None, ("seq", "tp"), None),
        P(None, "tp"),
        P(None, "tp"),
        P(None, "tp", None),
        P(None, "tp", None),
        P(None, "tp"),
        P(),
        P(),
    )
    out_specs = P("seq", None, "tp")
    return jax.shard_map(shards, mesh=mesh, in_specs=in_specs, out_specs=out_specs, check_vma=False)
```

```python
import jax
import jax.numpy as jnp
from jax import lax
from jax.sharding import PartitionSpec as P

HD = 256
ROT = 64
LAYERS = 2


def layer_norm(values, gain, shift):
    mean = jnp.mean(values, axis=-1, keepdims=True)
    centred = values - mean
    var = jnp.mean(centred * centred, axis=-1, keepdims=True)
    return centred * lax.rsqrt(var + 1e-05) * gain + shift


def positions(segs):
    length = segs.shape[-1]
    index = jnp.broadcast_to(jnp.arange(length, dtype=jnp.int32), segs.shape)
    first = jnp.ones(segs.shape[:-1] + (1,), dtype=bool)
    flag = jnp.concatenate([first, segs[..., 1:] != segs[..., :-1]], axis=-1)
    start = lax.cummax(jnp.where(flag, index, 0), axis=segs.ndim - 1)
    return index - start


def rotate(values, pos):
    half = ROT // 2
    inverse = 10000.0 ** (-(jnp.arange(half, dtype=jnp.float32) * 2.0 / ROT))
    angle = pos[..., None].astype(jnp.float32) * inverse
    cosine = jnp.cos(angle)[..., None, :]
    sine = jnp.sin(angle)[..., None, :]
    first = values[..., :half]
    second = values[..., half:ROT]
    return jnp.concatenate(
        [first * cosine - second * sine, second * cosine + first * sine, values[..., ROT:]], axis=-1
    )


def shards(
    tokens,
    segment_ids,
    shard_map,
    trainer_qkv,
    trainer_up,
    qkv_bias,
    up_bias,
    dense_w,
    down_w,
    out_bias,
    norm_gain,
    norm_shift,
):
    n_tp = lax.axis_size("tp")
    rows, length, _ = tokens.shape
    block = trainer_qkv.shape[1]
    full_width = block * n_tp * lax.axis_size("seq")
    n_blocks = full_width // block
    heads_here = qkv_bias.shape[1] // (3 * HD)
    qkv_cols = qkv_bias.shape[1]

    wq = trainer_qkv.astype(jnp.bfloat16).reshape(LAYERS, block, n_tp, qkv_cols)
    wu = trainer_up.astype(jnp.bfloat16).reshape(LAYERS, block, n_tp, up_bias.shape[1])
    packed = jnp.concatenate([wq, wu], axis=-1).transpose(0, 2, 1, 3).reshape(LAYERS, n_tp, -1)
    cols = packed.shape[2] // block
    width_here = tokens.shape[2]

    def exchange(x):
        return lax.all_to_all(x, "tp", split_axis=0, concat_axis=0, tiled=True)

    def spread(local):
        return jnp.broadcast_to(local.reshape(1, -1), (n_tp, local.size))

    def joined(got):
        got = got.reshape(n_tp, rows, length, width_here).transpose(1, 2, 0, 3)
        return got.reshape(rows, length, n_tp * width_here)

    pieces = [exchange(packed[layer]) for layer in range(LAYERS)]
    whole = joined(exchange(spread(tokens)))
    gathered = [lax.all_gather(piece.reshape(n_tp * block, cols), "seq", axis=0, tiled=True) for piece in pieces]

    pos = positions(segment_ids)
    index = jnp.arange(length, dtype=jnp.int32)
    mask = (index[None, :] <= index[:, None])[None] & (
        segment_ids[:, :, None] == segment_ids[:, None, :]
    )
    mask = mask[:, None]
    stream = tokens
    for layer in range(LAYERS):
        weights = gathered[layer]
        qkv_mat = weights[:, :qkv_cols]
        up_mat = weights[:, qkv_cols:]
        if layer > 0:
            whole = joined(exchange(spread(stream)))
        permuted = jnp.take(whole.reshape(rows, length, n_blocks, block), shard_map, axis=2)
        permuted = permuted.reshape(rows * length, full_width).astype(jnp.float32)

        def norm_of(i):
            gain = jnp.take(norm_gain[layer, i].reshape(n_blocks, block), shard_map, axis=0)
            shift = jnp.take(norm_shift[layer, i].reshape(n_blocks, block), shard_map, axis=0)
            return layer_norm(permuted, gain.reshape(-1), shift.reshape(-1)).astype(jnp.bfloat16)

        attn_in = norm_of(0)
        mlp_in = norm_of(1)
        qkv = jnp.dot(attn_in, qkv_mat, preferred_element_type=jnp.float32) + qkv_bias[layer].astype(jnp.float32)
        qkv = qkv.reshape(rows, length, heads_here, 3, HD)
        query = rotate(qkv[:, :, :, 0], pos).astype(jnp.bfloat16)
        keys = rotate(qkv[:, :, :, 1], pos).astype(jnp.bfloat16)
        vals = qkv[:, :, :, 2].astype(jnp.bfloat16)
        scores = jnp.einsum(
            "rqhd,rkhd->rhqk", query, keys, preferred_element_type=jnp.float32
        ) / jnp.sqrt(jnp.float32(HD))
        scores = jnp.where(mask, scores, -jnp.inf)
        probs = jax.nn.softmax(scores, axis=-1).astype(jnp.bfloat16)
        ctx = jnp.einsum("rhqk,rkhd->rqhd", probs, vals, preferred_element_type=jnp.float32).astype(
            jnp.bfloat16
        )
        ctx = ctx.reshape(rows * length, heads_here * HD)
        up = jnp.dot(mlp_in, up_mat, preferred_element_type=jnp.float32) + up_bias[layer].astype(jnp.float32)
        hidden_units = jax.nn.gelu(up, approximate=False).astype(jnp.bfloat16)
        partial_terms = jnp.dot(ctx, dense_w[layer], preferred_element_type=jnp.float32) + jnp.dot(
            hidden_units, down_w[layer], preferred_element_type=jnp.float32
        )
        partial_terms = partial_terms.astype(jnp.bfloat16)
        if layer + 1 < LAYERS:
            split = partial_terms.reshape(rows * length, n_tp, width_here).transpose(1, 0, 2)
            summed = jnp.sum(exchange(split).astype(jnp.float32), axis=0)
        else:
            summed = lax.psum_scatter(partial_terms, "tp", scatter_dimension=1, tiled=True).astype(jnp.float32)
        flat_stream = stream.astype(jnp.float32).reshape(rows * length, -1)
        stream = (flat_stream + summed + out_bias[layer]).astype(jnp.bfloat16).reshape(rows, length, -1)
    return stream


def solution(mesh):
    in_specs = (
        P("seq", None, "tp"),
        P("seq", None),
        P(),
        P(None, ("seq", "tp"), None),
        P(None, ("seq", "tp"), None),
        P(None, "tp"),
        P(None, "tp"),
        P(None, "tp", None),
        P(None, "tp", None),
        P(None, "tp"),
        P(),
        P(),
    )
    out_specs = P("seq", None, "tp")
    return jax.shard_map(shards, mesh=mesh, in_specs=in_specs, out_specs=out_specs, check_vma=False)
```

```python
import jax
import jax.numpy as jnp
from jax import lax
from jax.sharding import PartitionSpec as P

HD = 256
ROT = 64
LAYERS = 2


def layer_norm(values, gain, shift):
    mean = jnp.mean(values, axis=-1, keepdims=True)
    centred = values - mean
    var = jnp.mean(centred * centred, axis=-1, keepdims=True)
    return centred * lax.rsqrt(var + 1e-05) * gain + shift


def positions(segs):
    length = segs.shape[-1]
    index = jnp.broadcast_to(jnp.arange(length, dtype=jnp.int32), segs.shape)
    first = jnp.ones(segs.shape[:-1] + (1,), dtype=bool)
    flag = jnp.concatenate([first, segs[..., 1:] != segs[..., :-1]], axis=-1)
    start = lax.cummax(jnp.where(flag, index, 0), axis=segs.ndim - 1)
    return index - start


def rotate(values, pos):
    half = ROT // 2
    inverse = 10000.0 ** (-(jnp.arange(half, dtype=jnp.float32) * 2.0 / ROT))
    angle = pos[..., None].astype(jnp.float32) * inverse
    cosine = jnp.cos(angle)[..., None, :]
    sine = jnp.sin(angle)[..., None, :]
    first = values[..., :half]
    second = values[..., half:ROT]
    return jnp.concatenate(
        [first * cosine - second * sine, second * cosine + first * sine, values[..., ROT:]], axis=-1
    )


def shards(
    tokens,
    segment_ids,
    shard_map,
    trainer_qkv,
    trainer_up,
    qkv_bias,
    up_bias,
    dense_w,
    down_w,
    out_bias,
    norm_gain,
    norm_shift,
):
    n_tp = lax.axis_size("tp")
    rows, length, _ = tokens.shape
    block = trainer_qkv.shape[1]
    full_width = block * n_tp * lax.axis_size("seq")
    n_blocks = full_width // block
    heads_here = qkv_bias.shape[1] // (3 * HD)
    qkv_cols = qkv_bias.shape[1]

    wq = trainer_qkv.astype(jnp.bfloat16).reshape(LAYERS, block, n_tp, qkv_cols)
    wu = trainer_up.astype(jnp.bfloat16).reshape(LAYERS, block, n_tp, up_bias.shape[1])
    packed = jnp.concatenate([wq, wu], axis=-1)
    cols = packed.shape[3]
    width_here = tokens.shape[2]

    def exchange(x):
        return lax.all_to_all(x, "tp", split_axis=0, concat_axis=0, tiled=True)

    def spread(local):
        return jnp.broadcast_to(local.reshape(1, rows * length, width_here), (n_tp, rows * length, width_here))

    def joined(got):
        return got.transpose(1, 0, 2).reshape(rows, length, n_tp * width_here)

    pieces = [
        lax.all_to_all(packed[layer], "tp", split_axis=1, concat_axis=0, tiled=True) for layer in range(LAYERS)
    ]
    whole = joined(exchange(spread(tokens)))
    gathered = [lax.all_gather(piece.reshape(n_tp * block, cols), "seq", axis=0, tiled=True) for piece in pieces]

    pos = positions(segment_ids)
    index = jnp.arange(length, dtype=jnp.int32)
    mask = (index[None, :] <= index[:, None])[None] & (
        segment_ids[:, :, None] == segment_ids[:, None, :]
    )
    mask = mask[:, None]
    stream = tokens
    for layer in range(LAYERS):
        weights = gathered[layer]
        qkv_mat = weights[:, :qkv_cols]
        up_mat = weights[:, qkv_cols:]
        if layer > 0:
            whole = joined(exchange(spread(stream)))
        permuted = jnp.take(whole.reshape(rows, length, n_blocks, block), shard_map, axis=2)
        permuted = permuted.reshape(rows * length, full_width).astype(jnp.float32)

        def norm_of(i):
            gain = jnp.take(norm_gain[layer, i].reshape(n_blocks, block), shard_map, axis=0)
            shift = jnp.take(norm_shift[layer, i].reshape(n_blocks, block), shard_map, axis=0)
            return layer_norm(permuted, gain.reshape(-1), shift.reshape(-1)).astype(jnp.bfloat16)

        attn_in = norm_of(0)
        mlp_in = norm_of(1)
        qkv = jnp.dot(attn_in, qkv_mat, preferred_element_type=jnp.float32) + qkv_bias[layer].astype(jnp.float32)
        qkv = qkv.reshape(rows, length, heads_here, 3, HD)
        query = rotate(qkv[:, :, :, 0], pos).astype(jnp.bfloat16)
        keys = rotate(qkv[:, :, :, 1], pos).astype(jnp.bfloat16)
        vals = qkv[:, :, :, 2].astype(jnp.bfloat16)
        scores = jnp.einsum(
            "rqhd,rkhd->rhqk", query, keys, preferred_element_type=jnp.float32
        ) / jnp.sqrt(jnp.float32(HD))
        scores = jnp.where(mask, scores, -jnp.inf)
        probs = jax.nn.softmax(scores, axis=-1).astype(jnp.bfloat16)
        ctx = jnp.einsum("rhqk,rkhd->rqhd", probs, vals, preferred_element_type=jnp.float32).astype(
            jnp.bfloat16
        )
        ctx = ctx.reshape(rows * length, heads_here * HD)
        up = jnp.dot(mlp_in, up_mat, preferred_element_type=jnp.float32) + up_bias[layer].astype(jnp.float32)
        hidden_units = jax.nn.gelu(up, approximate=False).astype(jnp.bfloat16)
        partial_terms = jnp.dot(ctx, dense_w[layer], preferred_element_type=jnp.float32) + jnp.dot(
            hidden_units, down_w[layer], preferred_element_type=jnp.float32
        )
        partial_terms = partial_terms.astype(jnp.bfloat16)
        if layer + 1 < LAYERS:
            split = partial_terms.reshape(rows * length, n_tp, width_here).transpose(1, 0, 2)
            summed = jnp.sum(exchange(split).astype(jnp.float32), axis=0)
        else:
            summed = lax.psum_scatter(partial_terms, "tp", scatter_dimension=1, tiled=True).astype(jnp.float32)
        flat_stream = stream.astype(jnp.float32).reshape(rows * length, -1)
        stream = (flat_stream + summed + out_bias[layer]).astype(jnp.bfloat16).reshape(rows, length, -1)
    return stream


def solution(mesh):
    in_specs = (
        P("seq", None, "tp"),
        P("seq", None),
        P(),
        P(None, ("seq", "tp"), None),
        P(None, ("seq", "tp"), None),
        P(None, "tp"),
        P(None, "tp"),
        P(None, "tp", None),
        P(None, "tp", None),
        P(None, "tp"),
        P(),
        P(),
    )
    out_specs = P("seq", None, "tp")
    return jax.shard_map(shards, mesh=mesh, in_specs=in_specs, out_specs=out_specs, check_vma=False)
```

```python
import jax
import jax.numpy as jnp
from jax import lax
from jax.sharding import PartitionSpec as P

HD = 256
ROT = 64
LAYERS = 2


def layer_norm(values, gain, shift):
    mean = jnp.mean(values, axis=-1, keepdims=True)
    centred = values - mean
    var = jnp.mean(centred * centred, axis=-1, keepdims=True)
    return centred * lax.rsqrt(var + 1e-05) * gain + shift


def positions(segs):
    length = segs.shape[-1]
    index = jnp.broadcast_to(jnp.arange(length, dtype=jnp.int32), segs.shape)
    first = jnp.ones(segs.shape[:-1] + (1,), dtype=bool)
    flag = jnp.concatenate([first, segs[..., 1:] != segs[..., :-1]], axis=-1)
    start = lax.cummax(jnp.where(flag, index, 0), axis=segs.ndim - 1)
    return index - start


def rotate(values, pos):
    half = ROT // 2
    inverse = 10000.0 ** (-(jnp.arange(half, dtype=jnp.float32) * 2.0 / ROT))
    angle = pos[..., None].astype(jnp.float32) * inverse
    cosine = jnp.cos(angle)[..., None, :]
    sine = jnp.sin(angle)[..., None, :]
    first = values[..., :half]
    second = values[..., half:ROT]
    return jnp.concatenate(
        [first * cosine - second * sine, second * cosine + first * sine, values[..., ROT:]], axis=-1
    )


def shards(
    tokens,
    segment_ids,
    shard_map,
    trainer_qkv,
    trainer_up,
    qkv_bias,
    up_bias,
    dense_w,
    down_w,
    out_bias,
    norm_gain,
    norm_shift,
):
    n_tp = lax.axis_size("tp")
    rows, length, _ = tokens.shape
    block = trainer_qkv.shape[1]
    full_width = block * n_tp * lax.axis_size("seq")
    n_blocks = full_width // block
    heads_here = qkv_bias.shape[1] // (3 * HD)
    qkv_cols = qkv_bias.shape[1]

    wq = trainer_qkv.astype(jnp.bfloat16).reshape(LAYERS, block, n_tp, qkv_cols)
    wu = trainer_up.astype(jnp.bfloat16).reshape(LAYERS, block, n_tp, up_bias.shape[1])
    packed = jnp.concatenate([wq, wu], axis=-1)
    cols = packed.shape[3]
    width_here = tokens.shape[2]

    def exchange(x):
        return lax.all_to_all(x, "tp", split_axis=0, concat_axis=0, tiled=True)

    def spread(local):
        return jnp.broadcast_to(local.reshape(1, rows * length, width_here), (n_tp, rows * length, width_here))

    def joined(got):
        return got.transpose(1, 0, 2).reshape(rows, length, n_tp * width_here)

    pieces = [
        lax.all_to_all(packed[layer], "tp", split_axis=1, concat_axis=0, tiled=True) for layer in range(LAYERS)
    ]
    whole = joined(exchange(spread(tokens)))
    gathered = []
    for piece in pieces:
        piece = piece.reshape(n_tp * block, cols)
        gathered.append(
            [lax.all_gather(part, "seq", axis=0, tiled=True) for part in (piece[:, :qkv_cols], piece[:, qkv_cols:])]
        )

    pos = positions(segment_ids)
    index = jnp.arange(length, dtype=jnp.int32)
    mask = (index[None, :] <= index[:, None])[None] & (
        segment_ids[:, :, None] == segment_ids[:, None, :]
    )
    mask = mask[:, None]
    stream = tokens
    for layer in range(LAYERS):
        qkv_mat, up_mat = gathered[layer]
        if layer > 0:
            whole = joined(exchange(spread(stream)))
        permuted = jnp.take(whole.reshape(rows, length, n_blocks, block), shard_map, axis=2)
        permuted = permuted.reshape(rows * length, full_width).astype(jnp.float32)

        def norm_of(i):
            gain = jnp.take(norm_gain[layer, i].reshape(n_blocks, block), shard_map, axis=0)
            shift = jnp.take(norm_shift[layer, i].reshape(n_blocks, block), shard_map, axis=0)
            return layer_norm(permuted, gain.reshape(-1), shift.reshape(-1)).astype(jnp.bfloat16)

        attn_in = norm_of(0)
        mlp_in = norm_of(1)
        qkv = jnp.dot(attn_in, qkv_mat, preferred_element_type=jnp.float32) + qkv_bias[layer].astype(jnp.float32)
        qkv = qkv.reshape(rows, length, heads_here, 3, HD)
        query = rotate(qkv[:, :, :, 0], pos).astype(jnp.bfloat16)
        keys = rotate(qkv[:, :, :, 1], pos).astype(jnp.bfloat16)
        vals = qkv[:, :, :, 2].astype(jnp.bfloat16)
        scores = jnp.einsum(
            "rqhd,rkhd->rhqk", query, keys, preferred_element_type=jnp.float32
        ) / jnp.sqrt(jnp.float32(HD))
        scores = jnp.where(mask, scores, -jnp.inf)
        probs = jax.nn.softmax(scores, axis=-1).astype(jnp.bfloat16)
        ctx = jnp.einsum("rhqk,rkhd->rqhd", probs, vals, preferred_element_type=jnp.float32).astype(
            jnp.bfloat16
        )
        ctx = ctx.reshape(rows * length, heads_here * HD)
        up = jnp.dot(mlp_in, up_mat, preferred_element_type=jnp.float32) + up_bias[layer].astype(jnp.float32)
        hidden_units = jax.nn.gelu(up, approximate=False).astype(jnp.bfloat16)
        partial_terms = jnp.dot(ctx, dense_w[layer], preferred_element_type=jnp.float32) + jnp.dot(
            hidden_units, down_w[layer], preferred_element_type=jnp.float32
        )
        partial_terms = partial_terms.astype(jnp.bfloat16)
        split = partial_terms.reshape(rows * length, n_tp, width_here).transpose(1, 0, 2)
        summed = jnp.sum(exchange(split).astype(jnp.float32), axis=0)
        flat_stream = stream.astype(jnp.float32).reshape(rows * length, -1)
        stream = (flat_stream + summed + out_bias[layer]).astype(jnp.bfloat16).reshape(rows, length, -1)
    return stream


def solution(mesh):
    in_specs = (
        P("seq", None, "tp"),
        P("seq", None),
        P(),
        P(None, ("seq", "tp"), None),
        P(None, ("seq", "tp"), None),
        P(None, "tp"),
        P(None, "tp"),
        P(None, "tp", None),
        P(None, "tp", None),
        P(None, "tp"),
        P(),
        P(),
    )
    out_specs = P("seq", None, "tp")
    return jax.shard_map(shards, mesh=mesh, in_specs=in_specs, out_specs=out_specs, check_vma=False)
```

```python
import jax
import jax.numpy as jnp
from jax import lax
from jax.sharding import PartitionSpec as P

HD = 256
ROT = 64
LAYERS = 2


def layer_norm(values, gain, shift):
    mean = jnp.mean(values, axis=-1, keepdims=True)
    centred = values - mean
    var = jnp.mean(centred * centred, axis=-1, keepdims=True)
    return centred * lax.rsqrt(var + 1e-05) * gain + shift


def positions(segs):
    length = segs.shape[-1]
    index = jnp.broadcast_to(jnp.arange(length, dtype=jnp.int32), segs.shape)
    first = jnp.ones(segs.shape[:-1] + (1,), dtype=bool)
    flag = jnp.concatenate([first, segs[..., 1:] != segs[..., :-1]], axis=-1)
    start = lax.cummax(jnp.where(flag, index, 0), axis=segs.ndim - 1)
    return index - start


def rotate(values, pos):
    half = ROT // 2
    inverse = 10000.0 ** (-(jnp.arange(half, dtype=jnp.float32) * 2.0 / ROT))
    angle = pos[..., None].astype(jnp.float32) * inverse
    cosine = jnp.cos(angle)[..., None, :]
    sine = jnp.sin(angle)[..., None, :]
    first = values[..., :half]
    second = values[..., half:ROT]
    return jnp.concatenate(
        [first * cosine - second * sine, second * cosine + first * sine, values[..., ROT:]], axis=-1
    )


def shards(
    tokens,
    segment_ids,
    shard_map,
    trainer_qkv,
    trainer_up,
    qkv_bias,
    up_bias,
    dense_w,
    down_w,
    out_bias,
    norm_gain,
    norm_shift,
):
    n_tp = lax.axis_size("tp")
    rows, length, _ = tokens.shape
    block = trainer_qkv.shape[1]
    full_width = block * n_tp * lax.axis_size("seq")
    n_blocks = full_width // block
    heads_here = qkv_bias.shape[1] // (3 * HD)
    qkv_cols = qkv_bias.shape[1]

    wq = trainer_qkv.astype(jnp.bfloat16).reshape(LAYERS, block, n_tp, qkv_cols)
    wu = trainer_up.astype(jnp.bfloat16).reshape(LAYERS, block, n_tp, up_bias.shape[1])
    width_here = tokens.shape[2]

    def exchange(x):
        return lax.all_to_all(x, "tp", split_axis=0, concat_axis=0, tiled=True)

    def spread(local):
        return jnp.broadcast_to(local.reshape(1, rows * length, width_here), (n_tp, rows * length, width_here))

    def joined(got):
        return got.transpose(1, 0, 2).reshape(rows, length, n_tp * width_here)

    gathered = []
    for layer in range(LAYERS):
        parts = []
        for part in (wq[layer], wu[layer]):
            part = lax.all_to_all(part, "tp", split_axis=1, concat_axis=0, tiled=True)
            parts.append(lax.all_gather(part.reshape(n_tp * block, -1), "seq", axis=0, tiled=True))
        gathered.append(parts)
    whole = joined(exchange(spread(tokens)))

    pos = positions(segment_ids)
    index = jnp.arange(length, dtype=jnp.int32)
    mask = (index[None, :] <= index[:, None])[None] & (
        segment_ids[:, :, None] == segment_ids[:, None, :]
    )
    mask = mask[:, None]
    stream = tokens
    for layer in range(LAYERS):
        qkv_mat, up_mat = gathered[layer]
        if layer > 0:
            whole = joined(exchange(spread(stream)))
        permuted = jnp.take(whole.reshape(rows, length, n_blocks, block), shard_map, axis=2)
        permuted = permuted.reshape(rows * length, full_width).astype(jnp.float32)

        def norm_of(i):
            gain = jnp.take(norm_gain[layer, i].reshape(n_blocks, block), shard_map, axis=0)
            shift = jnp.take(norm_shift[layer, i].reshape(n_blocks, block), shard_map, axis=0)
            return layer_norm(permuted, gain.reshape(-1), shift.reshape(-1)).astype(jnp.bfloat16)

        attn_in = norm_of(0)
        mlp_in = norm_of(1)
        qkv = jnp.dot(attn_in, qkv_mat, preferred_element_type=jnp.float32) + qkv_bias[layer].astype(jnp.float32)
        qkv = qkv.reshape(rows, length, heads_here, 3, HD)
        query = rotate(qkv[:, :, :, 0], pos).astype(jnp.bfloat16)
        keys = rotate(qkv[:, :, :, 1], pos).astype(jnp.bfloat16)
        vals = qkv[:, :, :, 2].astype(jnp.bfloat16)
        scores = jnp.einsum(
            "rqhd,rkhd->rhqk", query, keys, preferred_element_type=jnp.float32
        ) / jnp.sqrt(jnp.float32(HD))
        scores = jnp.where(mask, scores, -jnp.inf)
        probs = jax.nn.softmax(scores, axis=-1).astype(jnp.bfloat16)
        ctx = jnp.einsum("rhqk,rkhd->rqhd", probs, vals, preferred_element_type=jnp.float32).astype(
            jnp.bfloat16
        )
        ctx = ctx.reshape(rows * length, heads_here * HD)
        up = jnp.dot(mlp_in, up_mat, preferred_element_type=jnp.float32) + up_bias[layer].astype(jnp.float32)
        hidden_units = jax.nn.gelu(up, approximate=False).astype(jnp.bfloat16)
        partial_terms = jnp.dot(ctx, dense_w[layer], preferred_element_type=jnp.float32) + jnp.dot(
            hidden_units, down_w[layer], preferred_element_type=jnp.float32
        )
        partial_terms = partial_terms.astype(jnp.bfloat16)
        split = partial_terms.reshape(rows * length, n_tp, width_here).transpose(1, 0, 2)
        summed = jnp.sum(exchange(split).astype(jnp.float32), axis=0)
        flat_stream = stream.astype(jnp.float32).reshape(rows * length, -1)
        stream = (flat_stream + summed + out_bias[layer]).astype(jnp.bfloat16).reshape(rows, length, -1)
    return stream


def solution(mesh):
    in_specs = (
        P("seq", None, "tp"),
        P("seq", None),
        P(),
        P(None, ("seq", "tp"), None),
        P(None, ("seq", "tp"), None),
        P(None, "tp"),
        P(None, "tp"),
        P(None, "tp", None),
        P(None, "tp", None),
        P(None, "tp"),
        P(),
        P(),
    )
    out_specs = P("seq", None, "tp")
    return jax.shard_map(shards, mesh=mesh, in_specs=in_specs, out_specs=out_specs, check_vma=False)
```

```python
import jax
import jax.numpy as jnp
from jax import lax
from jax.sharding import PartitionSpec as P

HD = 256
ROT = 64
LAYERS = 2


def layer_norm(values, gain, shift):
    mean = jnp.mean(values, axis=-1, keepdims=True)
    centred = values - mean
    var = jnp.mean(centred * centred, axis=-1, keepdims=True)
    return centred * lax.rsqrt(var + 1e-05) * gain + shift


def positions(segs):
    length = segs.shape[-1]
    index = jnp.broadcast_to(jnp.arange(length, dtype=jnp.int32), segs.shape)
    first = jnp.ones(segs.shape[:-1] + (1,), dtype=bool)
    flag = jnp.concatenate([first, segs[..., 1:] != segs[..., :-1]], axis=-1)
    start = lax.cummax(jnp.where(flag, index, 0), axis=segs.ndim - 1)
    return index - start


def rotate(values, pos):
    half = ROT // 2
    inverse = 10000.0 ** (-(jnp.arange(half, dtype=jnp.float32) * 2.0 / ROT))
    angle = pos[..., None].astype(jnp.float32) * inverse
    cosine = jnp.cos(angle)[..., None, :]
    sine = jnp.sin(angle)[..., None, :]
    first = values[..., :half]
    second = values[..., half:ROT]
    return jnp.concatenate(
        [first * cosine - second * sine, second * cosine + first * sine, values[..., ROT:]], axis=-1
    )


def shards(
    tokens,
    segment_ids,
    shard_map,
    trainer_qkv,
    trainer_up,
    qkv_bias,
    up_bias,
    dense_w,
    down_w,
    out_bias,
    norm_gain,
    norm_shift,
):
    n_tp = lax.axis_size("tp")
    rows, length, _ = tokens.shape
    block = trainer_qkv.shape[1]
    full_width = block * n_tp * lax.axis_size("seq")
    n_blocks = full_width // block
    heads_here = qkv_bias.shape[1] // (3 * HD)
    qkv_cols = qkv_bias.shape[1]

    wq = trainer_qkv.astype(jnp.bfloat16).reshape(LAYERS, block, n_tp, qkv_cols)
    wu = trainer_up.astype(jnp.bfloat16).reshape(LAYERS, block, n_tp, up_bias.shape[1])
    width_here = tokens.shape[2]

    def exchange(x):
        return lax.all_to_all(x, "tp", split_axis=0, concat_axis=0, tiled=True)

    def spread(local):
        return jnp.broadcast_to(local.reshape(1, rows * length, width_here), (n_tp, rows * length, width_here))

    def joined(got):
        return got.transpose(1, 0, 2).reshape(rows, length, n_tp * width_here)

    gathered = []
    for layer in range(LAYERS):
        parts = []
        for part in (wq[layer], wu[layer]):
            part = lax.all_to_all(part, "tp", split_axis=1, concat_axis=0, tiled=True)
            parts.append(lax.all_gather(part.reshape(n_tp * block, -1), "seq", axis=0, tiled=True))
        gathered.append(parts)
    whole = joined(exchange(spread(tokens)))

    pos = positions(segment_ids)
    index = jnp.arange(length, dtype=jnp.int32)
    mask = (index[None, :] <= index[:, None])[None] & (
        segment_ids[:, :, None] == segment_ids[:, None, :]
    )
    mask = mask[:, None]
    stream = tokens
    for layer in range(LAYERS):
        qkv_mat, up_mat = gathered[layer]
        if layer > 0:
            whole = joined(exchange(spread(stream)))
        permuted = jnp.take(whole.reshape(rows, length, n_blocks, block), shard_map, axis=2)
        permuted = permuted.reshape(rows * length, full_width).astype(jnp.float32)

        def norm_of(i):
            gain = jnp.take(norm_gain[layer, i].reshape(n_blocks, block), shard_map, axis=0)
            shift = jnp.take(norm_shift[layer, i].reshape(n_blocks, block), shard_map, axis=0)
            return layer_norm(permuted, gain.reshape(-1), shift.reshape(-1)).astype(jnp.bfloat16)

        attn_in = norm_of(0)
        mlp_in = norm_of(1)
        qkv = jnp.dot(attn_in, qkv_mat, preferred_element_type=jnp.float32) + qkv_bias[layer].astype(jnp.float32)
        qkv = qkv.reshape(rows, length, heads_here, 3, HD)
        query = rotate(qkv[:, :, :, 0], pos).astype(jnp.bfloat16)
        keys = rotate(qkv[:, :, :, 1], pos).astype(jnp.bfloat16)
        vals = qkv[:, :, :, 2].astype(jnp.bfloat16)
        scores = jnp.einsum(
            "rqhd,rkhd->rhqk", query, keys, preferred_element_type=jnp.float32
        ) / jnp.sqrt(jnp.float32(HD))
        scores = jnp.where(mask, scores, -jnp.inf)
        probs = jax.nn.softmax(scores, axis=-1).astype(jnp.bfloat16)
        ctx = jnp.einsum("rhqk,rkhd->rqhd", probs, vals, preferred_element_type=jnp.float32).astype(
            jnp.bfloat16
        )
        ctx = ctx.reshape(rows * length, heads_here * HD)
        chunks = 2 if layer + 1 == LAYERS else 1
        size = rows * length // chunks
        sums = []
        for chunk in range(chunks):
            rows_here = slice(chunk * size, (chunk + 1) * size)
            up = jnp.dot(mlp_in[rows_here], up_mat, preferred_element_type=jnp.float32)
            hidden_units = jax.nn.gelu(up + up_bias[layer].astype(jnp.float32), approximate=False).astype(jnp.bfloat16)
            partial_terms = jnp.dot(ctx[rows_here], dense_w[layer], preferred_element_type=jnp.float32) + jnp.dot(
                hidden_units, down_w[layer], preferred_element_type=jnp.float32
            )
            split = partial_terms.astype(jnp.bfloat16).reshape(size, n_tp, width_here).transpose(1, 0, 2)
            sums.append(jnp.sum(exchange(split).astype(jnp.float32), axis=0))
        summed = jnp.concatenate(sums, axis=0) if chunks > 1 else sums[0]
        flat_stream = stream.astype(jnp.float32).reshape(rows * length, -1)
        stream = (flat_stream + summed + out_bias[layer]).astype(jnp.bfloat16).reshape(rows, length, -1)
    return stream


def solution(mesh):
    in_specs = (
        P("seq", None, "tp"),
        P("seq", None),
        P(),
        P(None, ("seq", "tp"), None),
        P(None, ("seq", "tp"), None),
        P(None, "tp"),
        P(None, "tp"),
        P(None, "tp", None),
        P(None, "tp", None),
        P(None, "tp"),
        P(),
        P(),
    )
    out_specs = P("seq", None, "tp")
    return jax.shard_map(shards, mesh=mesh, in_specs=in_specs, out_specs=out_specs, check_vma=False)
```

```python
import jax
import jax.numpy as jnp
from jax import lax
from jax.sharding import PartitionSpec as P

HD = 256
ROT = 64
LAYERS = 2


def layer_norm(values, gain, shift):
    mean = jnp.mean(values, axis=-1, keepdims=True)
    centred = values - mean
    var = jnp.mean(centred * centred, axis=-1, keepdims=True)
    return centred * lax.rsqrt(var + 1e-05) * gain + shift


def positions(segs):
    length = segs.shape[-1]
    index = jnp.broadcast_to(jnp.arange(length, dtype=jnp.int32), segs.shape)
    first = jnp.ones(segs.shape[:-1] + (1,), dtype=bool)
    flag = jnp.concatenate([first, segs[..., 1:] != segs[..., :-1]], axis=-1)
    start = lax.cummax(jnp.where(flag, index, 0), axis=segs.ndim - 1)
    return index - start


def rotate(values, pos):
    half = ROT // 2
    inverse = 10000.0 ** (-(jnp.arange(half, dtype=jnp.float32) * 2.0 / ROT))
    angle = pos[..., None].astype(jnp.float32) * inverse
    cosine = jnp.cos(angle)[..., None, :]
    sine = jnp.sin(angle)[..., None, :]
    first = values[..., :half]
    second = values[..., half:ROT]
    return jnp.concatenate(
        [first * cosine - second * sine, second * cosine + first * sine, values[..., ROT:]], axis=-1
    )


def shards(
    tokens,
    segment_ids,
    shard_map,
    trainer_qkv,
    trainer_up,
    qkv_bias,
    up_bias,
    dense_w,
    down_w,
    out_bias,
    norm_gain,
    norm_shift,
):
    n_tp = lax.axis_size("tp")
    rows, length, _ = tokens.shape
    block = trainer_qkv.shape[1]
    full_width = block * n_tp * lax.axis_size("seq")
    n_blocks = full_width // block
    heads_here = qkv_bias.shape[1] // (3 * HD)
    qkv_cols = qkv_bias.shape[1]

    wq = trainer_qkv.astype(jnp.bfloat16).reshape(LAYERS, block, n_tp, qkv_cols)
    wu = trainer_up.astype(jnp.bfloat16).reshape(LAYERS, block, n_tp, up_bias.shape[1])
    width_here = tokens.shape[2]

    def exchange(x):
        return lax.all_to_all(x, "tp", split_axis=0, concat_axis=0, tiled=True)

    def spread(local):
        return jnp.broadcast_to(local.reshape(1, rows * length, width_here), (n_tp, rows * length, width_here))

    def joined(got):
        return got.transpose(1, 0, 2).reshape(rows, length, n_tp * width_here)

    ff_here = up_bias.shape[1]
    halves = [1] * (LAYERS - 1) + [2]

    def over_rows(part):
        part = lax.all_to_all(part, "tp", split_axis=1, concat_axis=0, tiled=True)
        return lax.all_gather(part.reshape(n_tp * block, -1), "seq", axis=0, tiled=True)

    gathered = []
    for layer in range(LAYERS):
        size = ff_here // halves[layer]
        ups = [over_rows(wu[layer][:, :, h * size : (h + 1) * size]) for h in range(halves[layer])]
        gathered.append((over_rows(wq[layer]), ups))
    whole = joined(exchange(spread(tokens)))

    pos = positions(segment_ids)
    index = jnp.arange(length, dtype=jnp.int32)
    mask = (index[None, :] <= index[:, None])[None] & (
        segment_ids[:, :, None] == segment_ids[:, None, :]
    )
    mask = mask[:, None]
    stream = tokens
    for layer in range(LAYERS):
        qkv_mat, up_mat = gathered[layer]
        if layer > 0:
            whole = joined(exchange(spread(stream)))
        permuted = jnp.take(whole.reshape(rows, length, n_blocks, block), shard_map, axis=2)
        permuted = permuted.reshape(rows * length, full_width).astype(jnp.float32)

        def norm_of(i):
            gain = jnp.take(norm_gain[layer, i].reshape(n_blocks, block), shard_map, axis=0)
            shift = jnp.take(norm_shift[layer, i].reshape(n_blocks, block), shard_map, axis=0)
            return layer_norm(permuted, gain.reshape(-1), shift.reshape(-1)).astype(jnp.bfloat16)

        attn_in = norm_of(0)
        mlp_in = norm_of(1)
        qkv = jnp.dot(attn_in, qkv_mat, preferred_element_type=jnp.float32) + qkv_bias[layer].astype(jnp.float32)
        qkv = qkv.reshape(rows, length, heads_here, 3, HD)
        query = rotate(qkv[:, :, :, 0], pos).astype(jnp.bfloat16)
        keys = rotate(qkv[:, :, :, 1], pos).astype(jnp.bfloat16)
        vals = qkv[:, :, :, 2].astype(jnp.bfloat16)
        scores = jnp.einsum(
            "rqhd,rkhd->rhqk", query, keys, preferred_element_type=jnp.float32
        ) / jnp.sqrt(jnp.float32(HD))
        scores = jnp.where(mask, scores, -jnp.inf)
        probs = jax.nn.softmax(scores, axis=-1).astype(jnp.bfloat16)
        ctx = jnp.einsum("rhqk,rkhd->rqhd", probs, vals, preferred_element_type=jnp.float32).astype(
            jnp.bfloat16
        )
        ctx = ctx.reshape(rows * length, heads_here * HD)
        partial_terms = jnp.dot(ctx, dense_w[layer], preferred_element_type=jnp.float32)
        size = ff_here // halves[layer]
        for h, up_part in enumerate(up_mat):
            units = slice(h * size, (h + 1) * size)
            up = jnp.dot(mlp_in, up_part, preferred_element_type=jnp.float32) + up_bias[layer, units].astype(jnp.float32)
            hidden_units = jax.nn.gelu(up, approximate=False).astype(jnp.bfloat16)
            partial_terms = partial_terms + jnp.dot(hidden_units, down_w[layer, units], preferred_element_type=jnp.float32)
        partial_terms = partial_terms.astype(jnp.bfloat16)
        split = partial_terms.reshape(rows * length, n_tp, width_here).transpose(1, 0, 2)
        summed = jnp.sum(exchange(split).astype(jnp.float32), axis=0)
        flat_stream = stream.astype(jnp.float32).reshape(rows * length, -1)
        stream = (flat_stream + summed + out_bias[layer]).astype(jnp.bfloat16).reshape(rows, length, -1)
    return stream


def solution(mesh):
    in_specs = (
        P("seq", None, "tp"),
        P("seq", None),
        P(),
        P(None, ("seq", "tp"), None),
        P(None, ("seq", "tp"), None),
        P(None, "tp"),
        P(None, "tp"),
        P(None, "tp", None),
        P(None, "tp", None),
        P(None, "tp"),
        P(),
        P(),
    )
    out_specs = P("seq", None, "tp")
    return jax.shard_map(shards, mesh=mesh, in_specs=in_specs, out_specs=out_specs, check_vma=False)
```

```python
import jax
import jax.numpy as jnp
from jax import lax
from jax.sharding import PartitionSpec as P

HD = 256
ROT = 64
LAYERS = 2


def layer_norm(values, gain, shift):
    mean = jnp.mean(values, axis=-1, keepdims=True)
    centred = values - mean
    var = jnp.mean(centred * centred, axis=-1, keepdims=True)
    return centred * lax.rsqrt(var + 1e-05) * gain + shift


def positions(segs):
    length = segs.shape[-1]
    index = jnp.broadcast_to(jnp.arange(length, dtype=jnp.int32), segs.shape)
    first = jnp.ones(segs.shape[:-1] + (1,), dtype=bool)
    flag = jnp.concatenate([first, segs[..., 1:] != segs[..., :-1]], axis=-1)
    start = lax.cummax(jnp.where(flag, index, 0), axis=segs.ndim - 1)
    return index - start


def rotate(values, pos):
    half = ROT // 2
    inverse = 10000.0 ** (-(jnp.arange(half, dtype=jnp.float32) * 2.0 / ROT))
    angle = pos[..., None].astype(jnp.float32) * inverse
    cosine = jnp.cos(angle)[..., None, :]
    sine = jnp.sin(angle)[..., None, :]
    first = values[..., :half]
    second = values[..., half:ROT]
    return jnp.concatenate(
        [first * cosine - second * sine, second * cosine + first * sine, values[..., ROT:]], axis=-1
    )


def shards(
    tokens,
    segment_ids,
    shard_map,
    trainer_qkv,
    trainer_up,
    qkv_bias,
    up_bias,
    dense_w,
    down_w,
    out_bias,
    norm_gain,
    norm_shift,
):
    n_tp = lax.axis_size("tp")
    rows, length, _ = tokens.shape
    block = trainer_qkv.shape[1]
    full_width = block * n_tp * lax.axis_size("seq")
    n_blocks = full_width // block
    heads_here = qkv_bias.shape[1] // (3 * HD)
    qkv_cols = qkv_bias.shape[1]

    wq = trainer_qkv.astype(jnp.bfloat16).reshape(LAYERS, block, n_tp, qkv_cols)
    wu = trainer_up.astype(jnp.bfloat16).reshape(LAYERS, block, n_tp, up_bias.shape[1])
    width_here = tokens.shape[2]

    def exchange(x):
        return lax.all_to_all(x, "tp", split_axis=0, concat_axis=0, tiled=True)

    def spread(local):
        return jnp.broadcast_to(local.reshape(1, rows * length, width_here), (n_tp, rows * length, width_here))

    def joined(got):
        return got.transpose(1, 0, 2).reshape(rows, length, n_tp * width_here)

    gathered = []
    for layer in range(LAYERS):
        parts = []
        for part in (wq[layer], wu[layer]):
            part = lax.all_to_all(part, "tp", split_axis=1, concat_axis=0, tiled=True)
            parts.append(lax.all_gather(part.reshape(n_tp * block, -1), "seq", axis=0, tiled=True))
        gathered.append(parts)
    whole = joined(exchange(spread(tokens)))

    pos = positions(segment_ids)
    index = jnp.arange(length, dtype=jnp.int32)
    mask = (index[None, :] <= index[:, None])[None] & (
        segment_ids[:, :, None] == segment_ids[:, None, :]
    )
    mask = mask[:, None]
    stream = tokens
    for layer in range(LAYERS):
        qkv_mat, up_mat = gathered[layer]
        if layer > 0:
            whole = joined(exchange(spread(stream)))
        permuted = jnp.take(whole.reshape(rows, length, n_blocks, block), shard_map, axis=2)
        permuted = permuted.reshape(rows * length, full_width).astype(jnp.float32)

        def norm_of(i):
            gain = jnp.take(norm_gain[layer, i].reshape(n_blocks, block), shard_map, axis=0)
            shift = jnp.take(norm_shift[layer, i].reshape(n_blocks, block), shard_map, axis=0)
            return layer_norm(permuted, gain.reshape(-1), shift.reshape(-1)).astype(jnp.bfloat16)

        attn_in = norm_of(0)
        mlp_in = norm_of(1)
        qkv = jnp.dot(attn_in, qkv_mat, preferred_element_type=jnp.float32) + qkv_bias[layer].astype(jnp.float32)
        qkv = qkv.reshape(rows, length, heads_here, 3, HD)
        query = rotate(qkv[:, :, :, 0], pos).astype(jnp.bfloat16)
        keys = rotate(qkv[:, :, :, 1], pos).astype(jnp.bfloat16)
        vals = qkv[:, :, :, 2].astype(jnp.bfloat16)
        scores = jnp.einsum(
            "rqhd,rkhd->rhqk", query, keys, preferred_element_type=jnp.float32
        ) / jnp.sqrt(jnp.float32(HD))
        scores = jnp.where(mask, scores, -jnp.inf)
        probs = jax.nn.softmax(scores, axis=-1).astype(jnp.bfloat16)
        ctx = jnp.einsum("rhqk,rkhd->rqhd", probs, vals, preferred_element_type=jnp.float32).astype(
            jnp.bfloat16
        )
        ctx = ctx.reshape(rows * length, heads_here * HD)
        up = jnp.dot(mlp_in, up_mat, preferred_element_type=jnp.float32) + up_bias[layer].astype(jnp.float32)
        hidden_units = jax.nn.gelu(up, approximate=False).astype(jnp.bfloat16)
        d_view = dense_w[layer].reshape(-1, n_tp, width_here)
        m_view = down_w[layer].reshape(-1, n_tp, width_here)
        split = jnp.einsum("tc,cgd->gtd", ctx, d_view, preferred_element_type=jnp.float32) + jnp.einsum(
            "th,hgd->gtd", hidden_units, m_view, preferred_element_type=jnp.float32
        )
        summed = jnp.sum(exchange(split.astype(jnp.bfloat16)).astype(jnp.float32), axis=0)
        flat_stream = stream.astype(jnp.float32).reshape(rows * length, -1)
        stream = (flat_stream + summed + out_bias[layer]).astype(jnp.bfloat16).reshape(rows, length, -1)
    return stream


def solution(mesh):
    in_specs = (
        P("seq", None, "tp"),
        P("seq", None),
        P(),
        P(None, ("seq", "tp"), None),
        P(None, ("seq", "tp"), None),
        P(None, "tp"),
        P(None, "tp"),
        P(None, "tp", None),
        P(None, "tp", None),
        P(None, "tp"),
        P(),
        P(),
    )
    out_specs = P("seq", None, "tp")
    return jax.shard_map(shards, mesh=mesh, in_specs=in_specs, out_specs=out_specs, check_vma=False)
```

```python
import jax
import jax.numpy as jnp
from jax import lax
from jax.sharding import PartitionSpec as P

HD = 256
ROT = 64
LAYERS = 2


def layer_norm(values, gain, shift):
    mean = jnp.mean(values, axis=-1, keepdims=True)
    centred = values - mean
    var = jnp.mean(centred * centred, axis=-1, keepdims=True)
    return centred * lax.rsqrt(var + 1e-05) * gain + shift


def positions(segs):
    length = segs.shape[-1]
    index = jnp.broadcast_to(jnp.arange(length, dtype=jnp.int32), segs.shape)
    first = jnp.ones(segs.shape[:-1] + (1,), dtype=bool)
    flag = jnp.concatenate([first, segs[..., 1:] != segs[..., :-1]], axis=-1)
    start = lax.cummax(jnp.where(flag, index, 0), axis=segs.ndim - 1)
    return index - start


def rotate(values, pos):
    half = ROT // 2
    inverse = 10000.0 ** (-(jnp.arange(half, dtype=jnp.float32) * 2.0 / ROT))
    angle = pos[..., None].astype(jnp.float32) * inverse
    cosine = jnp.cos(angle)[..., None, :]
    sine = jnp.sin(angle)[..., None, :]
    first = values[..., :half]
    second = values[..., half:ROT]
    return jnp.concatenate(
        [first * cosine - second * sine, second * cosine + first * sine, values[..., ROT:]], axis=-1
    )


def shards(
    tokens,
    segment_ids,
    shard_map,
    trainer_qkv,
    trainer_up,
    qkv_bias,
    up_bias,
    dense_w,
    down_w,
    out_bias,
    norm_gain,
    norm_shift,
):
    n_tp = lax.axis_size("tp")
    rows, length, _ = tokens.shape
    block = trainer_qkv.shape[1]
    full_width = block * n_tp * lax.axis_size("seq")
    n_blocks = full_width // block
    heads_here = qkv_bias.shape[1] // (3 * HD)
    qkv_cols = qkv_bias.shape[1]

    wq = trainer_qkv.astype(jnp.bfloat16).reshape(LAYERS, block, n_tp, qkv_cols)
    wu = trainer_up.astype(jnp.bfloat16).reshape(LAYERS, block, n_tp, up_bias.shape[1])
    width_here = tokens.shape[2]

    def exchange(x):
        return lax.all_to_all(x, "tp", split_axis=0, concat_axis=0, tiled=True)

    def spread(local):
        return jnp.broadcast_to(local.reshape(1, rows * length, width_here), (n_tp, rows * length, width_here))

    def joined(got):
        return got.transpose(1, 0, 2).reshape(rows, length, n_tp * width_here)

    gathered = []
    for layer in range(LAYERS):
        parts = []
        for part in (wq[layer], wu[layer]):
            part = lax.all_to_all(part, "tp", split_axis=1, concat_axis=0, tiled=True)
            parts.append(lax.all_gather(part.reshape(n_tp * block, -1), "seq", axis=0, tiled=True))
        gathered.append(parts)
    whole = joined(exchange(spread(tokens)))

    pos = positions(segment_ids)
    index = jnp.arange(length, dtype=jnp.int32)
    mask = (index[None, :] <= index[:, None])[None] & (
        segment_ids[:, :, None] == segment_ids[:, None, :]
    )
    mask = mask[:, None]
    stream = tokens
    for layer in range(LAYERS):
        qkv_mat, up_mat = gathered[layer]
        if layer > 0:
            whole = joined(exchange(spread(stream)))
        permuted = jnp.take(whole.reshape(rows, length, n_blocks, block), shard_map, axis=2)
        permuted = permuted.reshape(rows * length, full_width).astype(jnp.float32)

        def norm_of(i):
            gain = jnp.take(norm_gain[layer, i].reshape(n_blocks, block), shard_map, axis=0)
            shift = jnp.take(norm_shift[layer, i].reshape(n_blocks, block), shard_map, axis=0)
            return layer_norm(permuted, gain.reshape(-1), shift.reshape(-1)).astype(jnp.bfloat16)

        attn_in = norm_of(0)
        mlp_in = norm_of(1)
        qkv = jnp.dot(attn_in, qkv_mat, preferred_element_type=jnp.float32) + qkv_bias[layer].astype(jnp.float32)
        qkv = qkv.reshape(rows, length, heads_here, 3, HD)
        query = rotate(qkv[:, :, :, 0], pos).astype(jnp.bfloat16)
        keys = rotate(qkv[:, :, :, 1], pos).astype(jnp.bfloat16)
        vals = qkv[:, :, :, 2].astype(jnp.bfloat16)
        scores = jnp.einsum(
            "rqhd,rkhd->rhqk", query, keys, preferred_element_type=jnp.float32
        ) / jnp.sqrt(jnp.float32(HD))
        scores = jnp.where(mask, scores, -jnp.inf)
        probs = jax.nn.softmax(scores, axis=-1).astype(jnp.bfloat16)
        ctx = jnp.einsum("rhqk,rkhd->rqhd", probs, vals, preferred_element_type=jnp.float32).astype(
            jnp.bfloat16
        )
        ctx = ctx.reshape(rows * length, heads_here * HD)
        up = jnp.dot(mlp_in, up_mat, preferred_element_type=jnp.float32) + up_bias[layer].astype(jnp.float32)
        hidden_units = jax.nn.gelu(up, approximate=False).astype(jnp.bfloat16)
        chunks = 2 if layer + 1 == LAYERS else 1
        size = rows * length // chunks
        sums = []
        for chunk in range(chunks):
            part = slice(chunk * size, (chunk + 1) * size)
            partial_terms = jnp.dot(ctx[part], dense_w[layer], preferred_element_type=jnp.float32) + jnp.dot(
                hidden_units[part], down_w[layer], preferred_element_type=jnp.float32
            )
            split = partial_terms.astype(jnp.bfloat16).reshape(size, n_tp, width_here).transpose(1, 0, 2)
            sums.append(jnp.sum(exchange(split).astype(jnp.float32), axis=0))
        summed = jnp.concatenate(sums, axis=0) if chunks > 1 else sums[0]
        flat_stream = stream.astype(jnp.float32).reshape(rows * length, -1)
        stream = (flat_stream + summed + out_bias[layer]).astype(jnp.bfloat16).reshape(rows, length, -1)
    return stream


def solution(mesh):
    in_specs = (
        P("seq", None, "tp"),
        P("seq", None),
        P(),
        P(None, ("seq", "tp"), None),
        P(None, ("seq", "tp"), None),
        P(None, "tp"),
        P(None, "tp"),
        P(None, "tp", None),
        P(None, "tp", None),
        P(None, "tp"),
        P(),
        P(),
    )
    out_specs = P("seq", None, "tp")
    return jax.shard_map(shards, mesh=mesh, in_specs=in_specs, out_specs=out_specs, check_vma=False)
```
